32 devices in a mesh: groups: 2 (over y), gx: 4 (over z), gy: 4 (over x, core).
Axes of the slice: x: 2, y: 2, z: 4, core: 2. Of those that a mesh axis runs over, the one named last changes fastest.
Arguments:
- tokens: bfloat16 [40, 8192], P(('groups', 'gx'), 'gy'), parts along dimension 0, may hold values from -180 to 180, as said below
- norm_gain: float32 [8192], P('gy'), may hold values from 0.1 to 1.9
- w_gate: bfloat16 [8192, 24576], P('gy', 'gx'), may hold values from -0.0625 to 0.0625
- w_up: bfloat16 [8192, 24576], P('gy', 'gx'), may hold values from -0.0625 to 0.0625
- w_down: bfloat16 [24576, 8192], P('gx', 'gy'), may hold values from -0.0390625 to 0.0390625
Outputs:
- mixed: bfloat16 [40, 8192], P(('groups', 'gx'), 'gy'), parts along dimension 0
The draws below stay inside these ranges and needn't reach their ends.
There are 2 independent parts, one for each index of `groups`. The reference program is written for one: setup_inputs(seed, part) draws one part's arguments, and reference() takes and returns one part's arrays. A program takes and returns all parts, laid end to end along the dimension named above; an argument that names none is the same for every part. Nothing has to cross between parts.
Inputs may be any that keep to these rules, and one draw needn't show every extreme that they name: tokens are real-valued activations of order one to some tens.
All inputs are finite; a program needn't handle non-finite values.
Results may differ from the reference program's by a relative error of at most 0.0064.
Values may be sent and summed in bfloat16 or wider, within the bound.
No kernel may reach another device: no remote copies, remote signals or barrier semaphores. Data moves between devices by JAX's collectives and lax.ppermute only.
A program may use at most 192 MiB of HBM per device.

```python
import jax
import jax.numpy as jnp
from jax import lax

D = 8192
FF = 24576
TOKENS = 20


def draw_tokens(key, part):
    key_base, key_rows, key_cols = jax.random.split(key, 3)
    positions = jnp.arange(D, dtype=jnp.float32) / (D - 1)
    col_scale = jnp.exp(positions * jnp.log(3.0)) * jnp.exp(jax.random.uniform(key_cols, (D,), jnp.float32, -0.35, 0.35))
    row_scale = jnp.exp(jax.random.uniform(key_rows, (TOKENS, 1), jnp.float32, 0.0, jnp.log(10.0)))
    base = jnp.clip(jax.random.normal(key_base, (TOKENS, D), jnp.float32), -4.0, 4.0)
    return (base * row_scale * col_scale[None, :]).astype(jnp.bfloat16)


def block_scale(key, dims, cuts, least, top_value):
    level = 1.0
    for axis_at, shards_of in cuts:
        heights = jax.random.uniform(jax.random.fold_in(jax.random.fold_in(key, 6), axis_at), (shards_of,), jnp.float32, least / len(cuts), top_value / len(cuts))
        level = level * jnp.repeat(jnp.exp(heights), dims[axis_at] // shards_of).reshape((-1,) + (1,) * (len(dims) - 1 - axis_at))
    return level


def centred(stream_key, dims, spread, limit, shards=(), kind=jnp.bfloat16):
    gain = block_scale(stream_key, dims, shards, -0.22, 0.18) if shards else 1.0
    entries = jax.random.normal(stream_key, dims, jnp.float32) * spread * gain
    return jnp.minimum(jnp.maximum(entries, -limit), limit).astype(kind)


def setup_inputs(seed: int = 0, part: int = 0) -> dict:
    seeds = jax.random.split(jax.random.key(seed), 6)
    part_keys = jax.random.split(jax.random.fold_in(seeds[5], part), 6)
    return {
        "tokens": draw_tokens(jax.random.fold_in(jax.random.fold_in(seeds[5], part), 71), part),
        "norm_gain": jnp.clip(1.0 + 0.18 * jax.random.normal(seeds[1], (D,), jnp.float32), 0.1, 1.9),
        "w_gate": centred(seeds[2], (D, FF), D ** -0.5, 0.0625, ((0, 4), (1, 4))),
        "w_up": centred(seeds[3], (D, FF), D ** -0.5, 0.0625, ((0, 4), (1, 4))),
        "w_down": centred(seeds[4], (FF, D), FF ** -0.5, 0.0390625, ((0, 4), (1, 4))),
    }


epsilon = 1e-06

def reference(tokens, norm_gain, w_gate, w_up, w_down):
    values = tokens.astype(jnp.float32)
    inverse = lax.rsqrt(lax.optimization_barrier(jnp.mean(values * values, axis=1, keepdims=True)) + epsilon)
    normed = (values * inverse * norm_gain.astype(jnp.float32)[None, :]).astype(jnp.bfloat16)
    gate = jnp.dot(normed, w_gate, preferred_element_type=jnp.float32)
    up_part = jnp.dot(normed, w_up, preferred_element_type=jnp.float32)
    hidden = (jax.nn.silu(gate) * up_part).astype(jnp.bfloat16)
    return jnp.dot(hidden, w_down, preferred_element_type=jnp.float32).astype(jnp.bfloat16)
```

```python
import jax
import jax.numpy as jnp
from jax import lax
from jax.sharding import PartitionSpec as P


epsilon = 1e-06

FANOUT_MAX = 8
CHUNKS = 4


def fanout(x, axis, n):
    outs = [x]
    for k in range(1, n):
        outs.append(lax.ppermute(x, axis, [(a, (a + k) % n) for a in range(n)]))
    return outs


def gather_rows(normed, ngx):
    if ngx <= FANOUT_MAX:
        return jnp.concatenate(fanout(normed, "gx", ngx), axis=0)
    return lax.all_gather(normed, "gx", axis=0, tiled=True)


def scatter_rows(total, ngx):
    if ngx <= FANOUT_MAX:
        rows = total.shape[0] // ngx
        own = total[:rows]
        for m in range(1, ngx):
            k = (ngx - m) % ngx
            block = total[k * rows:(k + 1) * rows]
            own = own + lax.ppermute(block, "gx", [(a, (a + m) % ngx) for a in range(ngx)])
        return own
    return lax.psum_scatter(total, "gx", scatter_dimension=0, tiled=True)


def reduce_columns(both, ngy):
    if ngy <= FANOUT_MAX:
        me = lax.axis_index("gy")
        own = lax.dynamic_index_in_dim(both, me, axis=2, keepdims=False)
        for k in range(1, ngy):
            part = lax.dynamic_index_in_dim(both, (me + k) % ngy, axis=2, keepdims=False)
            own = own + lax.ppermute(part, "gy", [(a, (a + k) % ngy) for a in range(ngy)])
        return own
    return lax.psum_scatter(both, "gy", scatter_dimension=2, tiled=True)[:, :, 0]


def gather_columns(hidden, ngy):
    if ngy <= FANOUT_MAX:
        me = lax.axis_index("gy")
        stacked = jnp.stack(fanout(hidden, "gy", ngy), axis=0)
        order = (me - jnp.arange(ngy)) % ngy
        ordered = jnp.take(stacked, order, axis=0)
        return jnp.transpose(ordered, (1, 0, 2)).reshape(hidden.shape[0], -1)
    return lax.all_gather(hidden, "gy", axis=1, tiled=True)


def local(tokens, norm_gain, w_gate, w_up, w_down):
    ngx = lax.axis_size("gx")
    ngy = lax.axis_size("gy")
    features = tokens.shape[1] * ngy
    values = tokens.astype(jnp.float32)
    local_sq = jnp.sum(values * values, axis=1)
    if ngy <= FANOUT_MAX:
        total_sq = sum(fanout(local_sq, "gy", ngy))
    else:
        total_sq = lax.psum(local_sq, "gy")
    inverse = lax.rsqrt(total_sq / features + epsilon)
    normed = (values * inverse[:, None] * norm_gain[None, :]).astype(jnp.bfloat16)
    piece = gather_rows(normed, ngx)
    rows = piece.shape[0]

    width = w_gate.shape[1]
    chunks = CHUNKS if width % (CHUNKS * ngy * 128) == 0 else 1
    step = width // chunks
    total = None
    for c in range(chunks):
        cols = slice(c * step, (c + 1) * step)
        gate_part = jnp.dot(piece, w_gate[:, cols], preferred_element_type=jnp.float32)
        up_part = jnp.dot(piece, w_up[:, cols], preferred_element_type=jnp.float32)
        both = jnp.stack([gate_part, up_part]).reshape(2, rows, ngy, step // ngy)
        summed = reduce_columns(both, ngy)
        hidden = (jax.nn.silu(summed[0]) * summed[1]).astype(jnp.bfloat16)
        hidden_all = gather_columns(hidden, ngy)
        term = jnp.dot(hidden_all, w_down[cols, :], preferred_element_type=jnp.float32)
        total = term if total is None else total + term
    result = scatter_rows(total, ngx)
    return result.astype(jnp.bfloat16)


def solution(mesh):
    in_specs = (P(("groups", "gx"), "gy"), P("gy"), P("gy", "gx"), P("gy", "gx"), P("gx", "gy"))
    out_specs = P(("groups", "gx"), "gy")
    return jax.shard_map(local, mesh=mesh, in_specs=in_specs, out_specs=out_specs, check_vma=False)
```

```python
import jax
import jax.numpy as jnp
from jax import lax
from jax.sharding import PartitionSpec as P


epsilon = 1e-06

EXCHANGE_MAX = 8


def pairwise(n):
    return n <= EXCHANGE_MAX and n & (n - 1) == 0


def exchange(x, axis, n, s):
    return lax.ppermute(x, axis, [(a, a ^ (1 << s)) for a in range(n)])


def xor_reduce_scatter(x, axis, n, pos, bits):
    levels = n.bit_length() - 1
    me = lax.axis_index(axis)
    shape = x.shape
    x = x.reshape(shape[:pos] + (2,) * levels + (shape[pos] // n,) + shape[pos + 1:])
    remaining = list(range(levels - 1, -1, -1))
    for s in bits:
        at = pos + remaining.index(s)
        bit = (me >> s) & 1
        keep = lax.dynamic_index_in_dim(x, bit, axis=at, keepdims=False)
        send = lax.dynamic_index_in_dim(x, 1 - bit, axis=at, keepdims=False)
        x = keep + exchange(send, axis, n, s)
        remaining.remove(s)
    return x


def xor_all_gather(x, axis, n, pos, bits):
    levels = n.bit_length() - 1
    me = lax.axis_index(axis)
    have = []
    for s in bits:
        other = exchange(x, axis, n, s)
        at = pos + sum(1 for b in have if b > s)
        low = jnp.stack([x, other], axis=at)
        high = jnp.stack([other, x], axis=at)
        x = jnp.where(((me >> s) & 1) == 0, low, high)
        have.append(s)
    shape = x.shape
    return x.reshape(shape[:pos] + (-1,) + shape[pos + levels + 1:])


def xor_all_reduce(x, axis, n):
    for s in range(n.bit_length() - 1):
        x = x + exchange(x, axis, n, s)
    return x


def local(tokens, norm_gain, w_gate, w_up, w_down):
    ngx = lax.axis_size("gx")
    ngy = lax.axis_size("gy")
    features = tokens.shape[1] * ngy
    values = tokens.astype(jnp.float32)
    local_sq = jnp.sum(values * values, axis=1)
    if pairwise(ngy):
        total_sq = xor_all_reduce(local_sq, "gy", ngy)
    else:
        total_sq = lax.psum(local_sq, "gy")
    inverse = lax.rsqrt(total_sq / features + epsilon)
    normed = (values * inverse[:, None] * norm_gain[None, :]).astype(jnp.bfloat16)
    gx_levels = list(range(ngx.bit_length() - 1))
    if pairwise(ngx):
        piece = xor_all_gather(normed, "gx", ngx, 0, gx_levels[::-1])
    else:
        piece = lax.all_gather(normed, "gx", axis=0, tiled=True)

    gate_part = jnp.dot(piece, w_gate, preferred_element_type=jnp.float32)
    up_part = jnp.dot(piece, w_up, preferred_element_type=jnp.float32)
    both = jnp.stack([gate_part, up_part])
    gy_levels = list(range(ngy.bit_length() - 1))
    if pairwise(ngy):
        summed = xor_reduce_scatter(both, "gy", ngy, 2, gy_levels)
    else:
        summed = lax.psum_scatter(both, "gy", scatter_dimension=2, tiled=True)
    hidden = (jax.nn.silu(summed[0]) * summed[1]).astype(jnp.bfloat16)
    if pairwise(ngy):
        hidden_all = xor_all_gather(hidden, "gy", ngy, 1, gy_levels[::-1])
    else:
        hidden_all = lax.all_gather(hidden, "gy", axis=1, tiled=True)

    total = jnp.dot(hidden_all, w_down, preferred_element_type=jnp.float32)
    if pairwise(ngx):
        result = xor_reduce_scatter(total, "gx", ngx, 0, gx_levels)
    else:
        result = lax.psum_scatter(total, "gx", scatter_dimension=0, tiled=True)
    return result.astype(jnp.bfloat16)


def solution(mesh):
    in_specs = (P(("groups", "gx"), "gy"), P("gy"), P("gy", "gx"), P("gy", "gx"), P("gx", "gy"))
    out_specs = P(("groups", "gx"), "gy")
    return jax.shard_map(local, mesh=mesh, in_specs=in_specs, out_specs=out_specs, check_vma=False)
```

```python
import jax
import jax.numpy as jnp
from jax import lax
from jax.sharding import PartitionSpec as P


epsilon = 1e-06

EXCHANGE_MAX = 8


def pairwise(n):
    return n <= EXCHANGE_MAX and n & (n - 1) == 0


def exchange(x, axis, n, s):
    return lax.ppermute(x, axis, [(a, a ^ (1 << s)) for a in range(n)])


def xor_reduce_scatter(parts, axis, n, dim, bits):
    me = lax.axis_index(axis)
    for s in bits:
        bit = (me >> s) & 1
        half = parts[0].shape[dim] // 2
        keep = [lax.dynamic_slice_in_dim(p, bit * half, half, axis=dim) for p in parts]
        send = [lax.dynamic_slice_in_dim(p, (1 - bit) * half, half, axis=dim) for p in parts]
        got = exchange(jnp.stack(send), axis, n, s)
        parts = [k + got[i] for i, k in enumerate(keep)]
    return parts


def xor_all_gather(x, axis, n, dim, bits):
    me = lax.axis_index(axis)
    for s in bits:
        other = exchange(x, axis, n, s)
        low = jnp.concatenate([x, other], axis=dim)
        high = jnp.concatenate([other, x], axis=dim)
        x = jnp.where(((me >> s) & 1) == 0, low, high)
    return x


def xor_all_reduce(x, axis, n):
    for s in range(n.bit_length() - 1):
        x = x + exchange(x, axis, n, s)
    return x


def local(tokens, norm_gain, w_gate, w_up, w_down):
    ngx = lax.axis_size("gx")
    ngy = lax.axis_size("gy")
    features = tokens.shape[1] * ngy
    values = tokens.astype(jnp.float32)
    local_sq = jnp.sum(values * values, axis=1)
    if pairwise(ngy):
        total_sq = xor_all_reduce(local_sq, "gy", ngy)
    else:
        total_sq = lax.psum(local_sq, "gy")
    inverse = lax.rsqrt(total_sq / features + epsilon)
    normed = (values * inverse[:, None] * norm_gain[None, :]).astype(jnp.bfloat16)
    gx_levels = list(range(ngx.bit_length() - 1))
    if pairwise(ngx):
        piece = xor_all_gather(normed, "gx", ngx, 0, gx_levels[::-1])
    else:
        piece = lax.all_gather(normed, "gx", axis=0, tiled=True)

    gate_part = jnp.dot(piece, w_gate, preferred_element_type=jnp.float32)
    up_part = jnp.dot(piece, w_up, preferred_element_type=jnp.float32)
    gy_levels = list(range(ngy.bit_length() - 1))
    if pairwise(ngy):
        gate, up = xor_reduce_scatter([gate_part, up_part], "gy", ngy, 1, gy_levels)
    else:
        gate = lax.psum_scatter(gate_part, "gy", scatter_dimension=1, tiled=True)
        up = lax.psum_scatter(up_part, "gy", scatter_dimension=1, tiled=True)
    hidden = (jax.nn.silu(gate) * up).astype(jnp.bfloat16)
    if pairwise(ngy):
        hidden_all = xor_all_gather(hidden, "gy", ngy, 1, gy_levels[::-1])
    else:
        hidden_all = lax.all_gather(hidden, "gy", axis=1, tiled=True)

    total = jnp.dot(hidden_all, w_down, preferred_element_type=jnp.float32)
    if pairwise(ngx):
        (result,) = xor_reduce_scatter([total], "gx", ngx, 0, gx_levels)
    else:
        result = lax.psum_scatter(total, "gx", scatter_dimension=0, tiled=True)
    return result.astype(jnp.bfloat16)


def solution(mesh):
    in_specs = (P(("groups", "gx"), "gy"), P("gy"), P("gy", "gx"), P("gy", "gx"), P("gx", "gy"))
    out_specs = P(("groups", "gx"), "gy")
    return jax.shard_map(local, mesh=mesh, in_specs=in_specs, out_specs=out_specs, check_vma=False)
```

```python
import jax
import jax.numpy as jnp
from jax import lax
from jax.sharding import PartitionSpec as P


epsilon = 1e-06

EXCHANGE_MAX = 8


def pairwise(n):
    return n <= EXCHANGE_MAX and n & (n - 1) == 0


def exchange(x, axis, n, s):
    return lax.ppermute(x, axis, [(a, a ^ (1 << s)) for a in range(n)])


def xor_reduce_scatter(parts, axis, n, dim, bits):
    me = lax.axis_index(axis)
    for s in bits:
        bit = (me >> s) & 1
        half = parts[0].shape[dim] // 2
        keep = [lax.dynamic_slice_in_dim(p, bit * half, half, axis=dim) for p in parts]
        send = [lax.dynamic_slice_in_dim(p, (1 - bit) * half, half, axis=dim) for p in parts]
        got = exchange(jnp.stack(send), axis, n, s)
        parts = [k + got[i] for i, k in enumerate(keep)]
    return parts


def xor_all_gather(x, axis, n, dim, bits):
    me = lax.axis_index(axis)
    for s in bits:
        other = exchange(x, axis, n, s)
        low = jnp.concatenate([x, other], axis=dim)
        high = jnp.concatenate([other, x], axis=dim)
        x = jnp.where(((me >> s) & 1) == 0, low, high)
    return x


def xor_all_reduce(x, axis, n):
    for s in range(n.bit_length() - 1):
        x = x + exchange(x, axis, n, s)
    return x


def spread(x, axis, n):
    return lax.all_to_all(x, axis, 0, 0, tiled=True)


def local(tokens, norm_gain, w_gate, w_up, w_down):
    ngx = lax.axis_size("gx")
    ngy = lax.axis_size("gy")
    rows_here, width_here = tokens.shape
    features = width_here * ngy
    if ngx * ngy <= 4 * EXCHANGE_MAX:
        copies = jnp.broadcast_to(tokens[None], (ngx * ngy,) + tokens.shape)
        every = spread(copies, ("gx", "gy"), ngx * ngy).reshape(ngx, ngy, rows_here, width_here)
        values_all = every.astype(jnp.float32)
        total_sq = jnp.sum(values_all * values_all, axis=(1, 3)).reshape(-1)
        mine = lax.dynamic_index_in_dim(every, lax.axis_index("gy"), axis=1, keepdims=False)
        values = mine.reshape(ngx * rows_here, width_here).astype(jnp.float32)
        inverse = lax.rsqrt(total_sq / features + epsilon)
        piece = (values * inverse[:, None] * norm_gain[None, :]).astype(jnp.bfloat16)
    else:
        values = tokens.astype(jnp.float32)
        total_sq = lax.psum(jnp.sum(values * values, axis=1), "gy")
        inverse = lax.rsqrt(total_sq / features + epsilon)
        normed = (values * inverse[:, None] * norm_gain[None, :]).astype(jnp.bfloat16)
        piece = lax.all_gather(normed, "gx", axis=0, tiled=True)
    rows = piece.shape[0]

    gate_part = jnp.dot(piece, w_gate, preferred_element_type=jnp.float32)
    up_part = jnp.dot(piece, w_up, preferred_element_type=jnp.float32)
    width = w_gate.shape[1]
    block = width // ngy
    if ngy <= EXCHANGE_MAX:
        both = jnp.stack([gate_part, up_part])
        blocks = jnp.stack([both[:, :, k * block:(k + 1) * block] for k in range(ngy)])
        summed = jnp.sum(spread(blocks, "gy", ngy), axis=0)
        hidden = (jax.nn.silu(summed[0]) * summed[1]).astype(jnp.bfloat16)
        copies = jnp.broadcast_to(hidden[None], (ngy,) + hidden.shape)
        hidden_all = jnp.transpose(spread(copies, "gy", ngy), (1, 0, 2)).reshape(rows, width)
    else:
        gate = lax.psum_scatter(gate_part, "gy", scatter_dimension=1, tiled=True)
        up = lax.psum_scatter(up_part, "gy", scatter_dimension=1, tiled=True)
        hidden = (jax.nn.silu(gate) * up).astype(jnp.bfloat16)
        hidden_all = lax.all_gather(hidden, "gy", axis=1, tiled=True)

    total = jnp.dot(hidden_all, w_down, preferred_element_type=jnp.float32)
    if ngx <= EXCHANGE_MAX:
        parts = spread(total.reshape(ngx, rows // ngx, -1), "gx", ngx)
        result = jnp.sum(parts, axis=0)
    else:
        result = lax.psum_scatter(total, "gx", scatter_dimension=0, tiled=True)
    return result.astype(jnp.bfloat16)


def solution(mesh):
    in_specs = (P(("groups", "gx"), "gy"), P("gy"), P("gy", "gx"), P("gy", "gx"), P("gx", "gy"))
    out_specs = P(("groups", "gx"), "gy")
    return jax.shard_map(local, mesh=mesh, in_specs=in_specs, out_specs=out_specs, check_vma=False)
```

```python
import jax
import jax.numpy as jnp
from jax import lax
from jax.sharding import PartitionSpec as P


epsilon = 1e-06

EXCHANGE_MAX = 8
CHUNKS = 2


def pairwise(n):
    return n <= EXCHANGE_MAX and n & (n - 1) == 0


def exchange(x, axis, n, s):
    return lax.ppermute(x, axis, [(a, a ^ (1 << s)) for a in range(n)])


def xor_reduce_scatter(parts, axis, n, dim, bits):
    me = lax.axis_index(axis)
    for s in bits:
        bit = (me >> s) & 1
        half = parts[0].shape[dim] // 2
        keep = [lax.dynamic_slice_in_dim(p, bit * half, half, axis=dim) for p in parts]
        send = [lax.dynamic_slice_in_dim(p, (1 - bit) * half, half, axis=dim) for p in parts]
        got = exchange(jnp.stack(send), axis, n, s)
        parts = [k + got[i] for i, k in enumerate(keep)]
    return parts


def xor_all_gather(x, axis, n, dim, bits):
    me = lax.axis_index(axis)
    for s in bits:
        other = exchange(x, axis, n, s)
        low = jnp.concatenate([x, other], axis=dim)
        high = jnp.concatenate([other, x], axis=dim)
        x = jnp.where(((me >> s) & 1) == 0, low, high)
    return x


def xor_all_reduce(x, axis, n):
    for s in range(n.bit_length() - 1):
        x = x + exchange(x, axis, n, s)
    return x


def local(tokens, norm_gain, w_gate, w_up, w_down):
    ngx = lax.axis_size("gx")
    ngy = lax.axis_size("gy")
    features = tokens.shape[1] * ngy
    values = tokens.astype(jnp.float32)
    local_sq = jnp.sum(values * values, axis=1)
    if pairwise(ngy):
        total_sq = xor_all_reduce(local_sq, "gy", ngy)
    else:
        total_sq = lax.psum(local_sq, "gy")
    inverse = lax.rsqrt(total_sq / features + epsilon)
    normed = (values * inverse[:, None] * norm_gain[None, :]).astype(jnp.bfloat16)
    gx_levels = list(range(ngx.bit_length() - 1))
    if pairwise(ngx):
        piece = xor_all_gather(normed, "gx", ngx, 0, gx_levels[::-1])
    else:
        piece = lax.all_gather(normed, "gx", axis=0, tiled=True)

    width = w_gate.shape[1]
    chunks = CHUNKS if width % (CHUNKS * ngy * 128) == 0 else 1
    step = width // chunks
    gy_levels = list(range(ngy.bit_length() - 1))
    total = None
    for c in range(chunks):
        cols = slice(c * step, (c + 1) * step)
        gate_part = jnp.dot(piece, w_gate[:, cols], preferred_element_type=jnp.float32)
        up_part = jnp.dot(piece, w_up[:, cols], preferred_element_type=jnp.float32)
        if pairwise(ngy):
            gate, up = xor_reduce_scatter([gate_part, up_part], "gy", ngy, 1, gy_levels)
        else:
            gate = lax.psum_scatter(gate_part, "gy", scatter_dimension=1, tiled=True)
            up = lax.psum_scatter(up_part, "gy", scatter_dimension=1, tiled=True)
        hidden = (jax.nn.silu(gate) * up).astype(jnp.bfloat16)
        if pairwise(ngy):
            hidden_all = xor_all_gather(hidden, "gy", ngy, 1, gy_levels[::-1])
        else:
            hidden_all = lax.all_gather(hidden, "gy", axis=1, tiled=True)
        term = jnp.dot(hidden_all, w_down[cols, :], preferred_element_type=jnp.float32)
        total = term if total is None else total + term
    if pairwise(ngx):
        (result,) = xor_reduce_scatter([total], "gx", ngx, 0, gx_levels)
    else:
        result = lax.psum_scatter(total, "gx", scatter_dimension=0, tiled=True)
    return result.astype(jnp.bfloat16)


def solution(mesh):
    in_specs = (P(("groups", "gx"), "gy"), P("gy"), P("gy", "gx"), P("gy", "gx"), P("gx", "gy"))
    out_specs = P(("groups", "gx"), "gy")
    return jax.shard_map(local, mesh=mesh, in_specs=in_specs, out_specs=out_specs, check_vma=False)
```

```python
import jax
import jax.numpy as jnp
from jax import lax
from jax.sharding import PartitionSpec as P


epsilon = 1e-06

EXCHANGE_MAX = 8
CHUNKS = 2


def pairwise(n):
    return n <= EXCHANGE_MAX and n & (n - 1) == 0


def exchange(x, axis, n, s):
    return lax.ppermute(x, axis, [(a, a ^ (1 << s)) for a in range(n)])


def xor_reduce_scatter(parts, axis, n, dim, bits):
    me = lax.axis_index(axis)
    for s in bits:
        bit = (me >> s) & 1
        half = parts[0].shape[dim] // 2
        keep = [lax.dynamic_slice_in_dim(p, bit * half, half, axis=dim) for p in parts]
        send = [lax.dynamic_slice_in_dim(p, (1 - bit) * half, half, axis=dim) for p in parts]
        got = exchange(jnp.stack(send), axis, n, s)
        parts = [k + got[i] for i, k in enumerate(keep)]
    return parts


def xor_all_gather(x, axis, n, dim, bits):
    me = lax.axis_index(axis)
    for s in bits:
        other = exchange(x, axis, n, s)
        low = jnp.concatenate([x, other], axis=dim)
        high = jnp.concatenate([other, x], axis=dim)
        x = jnp.where(((me >> s) & 1) == 0, low, high)
    return x


def xor_all_reduce(x, axis, n):
    for s in range(n.bit_length() - 1):
        x = x + exchange(x, axis, n, s)
    return x


def gathered_position(d, bits):
    return sum(((d >> s) & 1) << t for t, s in enumerate(bits))


def fanout_reduce_scatter(x, axis, n, bits):
    me = lax.axis_index(axis)
    rows = x.shape[0] // n
    own = lax.dynamic_slice_in_dim(x, gathered_position(me, bits) * rows, rows, axis=0)
    for k in range(1, n):
        block = lax.dynamic_slice_in_dim(x, gathered_position(me ^ k, bits) * rows, rows, axis=0)
        own = own + lax.ppermute(block, axis, [(a, a ^ k) for a in range(n)])
    return own


def local(tokens, norm_gain, w_gate, w_up, w_down):
    ngx = lax.axis_size("gx")
    ngy = lax.axis_size("gy")
    features = tokens.shape[1] * ngy
    gx_levels = list(range(ngx.bit_length() - 1))
    if pairwise(ngx):
        raw = xor_all_gather(tokens, "gx", ngx, 0, gx_levels[::-1])
    else:
        raw = lax.all_gather(tokens, "gx", axis=0, tiled=True)
    values = raw.astype(jnp.float32)
    piece = (values * norm_gain[None, :]).astype(jnp.bfloat16)
    local_sq = jnp.sum(values * values, axis=1)
    if pairwise(ngy):
        total_sq = xor_all_reduce(local_sq, "gy", ngy)
    else:
        total_sq = lax.psum(local_sq, "gy")
    inverse = lax.rsqrt(total_sq / features + epsilon)[:, None]
    rows = piece.shape[0]

    width = w_gate.shape[1]
    chunks = CHUNKS if width % (CHUNKS * ngy * 128) == 0 else 1
    step = width // chunks
    gy_levels = list(range(ngy.bit_length() - 1))
    total = None
    for c in range(chunks):
        cols = slice(c * step, (c + 1) * step)
        gate_part = jnp.dot(piece, w_gate[:, cols], preferred_element_type=jnp.float32)
        up_part = jnp.dot(piece, w_up[:, cols], preferred_element_type=jnp.float32)
        if pairwise(ngy):
            gate, up = xor_reduce_scatter([gate_part, up_part], "gy", ngy, 1, gy_levels)
        else:
            gate = lax.psum_scatter(gate_part, "gy", scatter_dimension=1, tiled=True)
            up = lax.psum_scatter(up_part, "gy", scatter_dimension=1, tiled=True)
        hidden = (jax.nn.silu(gate * inverse) * (up * inverse)).astype(jnp.bfloat16)
        if pairwise(ngy):
            hidden_all = xor_all_gather(hidden, "gy", ngy, 1, gy_levels[::-1])
        else:
            hidden_all = lax.all_gather(hidden, "gy", axis=1, tiled=True)
        term = jnp.dot(hidden_all, w_down[cols, :], preferred_element_type=jnp.float32)
        total = term if total is None else total + term
    if pairwise(ngx):
        result = fanout_reduce_scatter(total, "gx", ngx, gx_levels[::-1])
    else:
        result = lax.psum_scatter(total, "gx", scatter_dimension=0, tiled=True)
    return result.astype(jnp.bfloat16)


def solution(mesh):
    in_specs = (P(("groups", "gx"), "gy"), P("gy"), P("gy", "gx"), P("gy", "gx"), P("gx", "gy"))
    out_specs = P(("groups", "gx"), "gy")
    return jax.shard_map(local, mesh=mesh, in_specs=in_specs, out_specs=out_specs, check_vma=False)
```

```python
import jax
import jax.numpy as jnp
from jax import lax
from jax.sharding import PartitionSpec as P


epsilon = 1e-06

EXCHANGE_MAX = 8
CHUNKS = 2


def pairwise(n):
    return n <= EXCHANGE_MAX and n & (n - 1) == 0


def exchange(x, axis, n, s):
    return lax.ppermute(x, axis, [(a, a ^ (1 << s)) for a in range(n)])


def xor_reduce_scatter(parts, axis, n, dim, bits):
    me = lax.axis_index(axis)
    for s in bits:
        bit = (me >> s) & 1
        half = parts[0].shape[dim] // 2
        keep = [lax.dynamic_slice_in_dim(p, bit * half, half, axis=dim) for p in parts]
        send = [lax.dynamic_slice_in_dim(p, (1 - bit) * half, half, axis=dim) for p in parts]
        got = exchange(jnp.stack(send), axis, n, s)
        parts = [k + got[i] for i, k in enumerate(keep)]
    return parts


def xor_all_gather(x, axis, n, dim, bits):
    me = lax.axis_index(axis)
    for s in bits:
        other = exchange(x, axis, n, s)
        low = jnp.concatenate([x, other], axis=dim)
        high = jnp.concatenate([other, x], axis=dim)
        x = jnp.where(((me >> s) & 1) == 0, low, high)
    return x


def xor_all_reduce(x, axis, n):
    for s in range(n.bit_length() - 1):
        x = x + exchange(x, axis, n, s)
    return x


def gathered_position(d, bits):
    return sum(((d >> s) & 1) << t for t, s in enumerate(bits))


def fanout_reduce_scatter(x, axis, n, bits):
    me = lax.axis_index(axis)
    rows = x.shape[0] // n
    own = lax.dynamic_slice_in_dim(x, gathered_position(me, bits) * rows, rows, axis=0)
    for k in range(1, n):
        block = lax.dynamic_slice_in_dim(x, gathered_position(me ^ k, bits) * rows, rows, axis=0)
        own = own + lax.ppermute(block, axis, [(a, a ^ k) for a in range(n)])
    return own


def local(tokens, norm_gain, w_gate, w_up, w_down):
    ngx = lax.axis_size("gx")
    ngy = lax.axis_size("gy")
    features = tokens.shape[1] * ngy
    gx_levels = list(range(ngx.bit_length() - 1))
    if pairwise(ngx):
        raw = xor_all_gather(tokens, "gx", ngx, 0, gx_levels[::-1])
    else:
        raw = lax.all_gather(tokens, "gx", axis=0, tiled=True)
    values = raw.astype(jnp.float32)
    local_sq = jnp.sum(values * values, axis=1)
    if pairwise(ngy):
        total_sq = xor_all_reduce(local_sq, "gy", ngy)
    else:
        total_sq = lax.psum(local_sq, "gy")
    inverse = lax.rsqrt(total_sq / features + epsilon)
    piece = (values * inverse[:, None] * norm_gain[None, :]).astype(jnp.bfloat16)
    rows = piece.shape[0]

    width = w_gate.shape[1]
    chunks = CHUNKS if width % (CHUNKS * ngy * 128) == 0 else 1
    step = width // chunks
    gy_levels = list(range(ngy.bit_length() - 1))
    total = None
    for c in range(chunks):
        cols = slice(c * step, (c + 1) * step)
        gate_part = jnp.dot(piece, w_gate[:, cols], preferred_element_type=jnp.float32)
        up_part = jnp.dot(piece, w_up[:, cols], preferred_element_type=jnp.float32)
        if pairwise(ngy):
            gate, up = xor_reduce_scatter([gate_part, up_part], "gy", ngy, 1, gy_levels)
        else:
            gate = lax.psum_scatter(gate_part, "gy", scatter_dimension=1, tiled=True)
            up = lax.psum_scatter(up_part, "gy", scatter_dimension=1, tiled=True)
        hidden = (jax.nn.silu(gate) * up).astype(jnp.bfloat16)
        if pairwise(ngy):
            hidden_all = xor_all_gather(hidden, "gy", ngy, 1, gy_levels[::-1])
        else:
            hidden_all = lax.all_gather(hidden, "gy", axis=1, tiled=True)
        term = jnp.dot(hidden_all, w_down[cols, :], preferred_element_type=jnp.float32)
        total = term if total is None else total + term
    if pairwise(ngx):
        result = fanout_reduce_scatter(total, "gx", ngx, gx_levels[::-1])
    else:
        result = lax.psum_scatter(total, "gx", scatter_dimension=0, tiled=True)
    return result.astype(jnp.bfloat16)


def solution(mesh):
    in_specs = (P(("groups", "gx"), "gy"), P("gy"), P("gy", "gx"), P("gy", "gx"), P("gx", "gy"))
    out_specs = P(("groups", "gx"), "gy")
    return jax.shard_map(local, mesh=mesh, in_specs=in_specs, out_specs=out_specs, check_vma=False)
```

```python
import jax
import jax.numpy as jnp
from jax import lax
from jax.experimental import pallas as pl
from jax.experimental.pallas import tpu as pltpu
from jax.sharding import PartitionSpec as P


epsilon = 1e-06

EXCHANGE_MAX = 8
CHUNKS = 2
TILE = 768


def pairwise(n):
    return n <= EXCHANGE_MAX and n & (n - 1) == 0


def exchange(x, axis, n, s):
    return lax.ppermute(x, axis, [(a, a ^ (1 << s)) for a in range(n)])


def xor_reduce_scatter(parts, axis, n, dim, bits):
    me = lax.axis_index(axis)
    for s in bits:
        bit = (me >> s) & 1
        half = parts[0].shape[dim] // 2
        keep = [lax.dynamic_slice_in_dim(p, bit * half, half, axis=dim) for p in parts]
        send = [lax.dynamic_slice_in_dim(p, (1 - bit) * half, half, axis=dim) for p in parts]
        got = exchange(jnp.stack(send), axis, n, s)
        parts = [k + got[i] for i, k in enumerate(keep)]
    return parts


def xor_all_gather(x, axis, n, dim, bits):
    me = lax.axis_index(axis)
    for s in bits:
        other = exchange(x, axis, n, s)
        low = jnp.concatenate([x, other], axis=dim)
        high = jnp.concatenate([other, x], axis=dim)
        x = jnp.where(((me >> s) & 1) == 0, low, high)
    return x


def xor_all_reduce(x, axis, n):
    for s in range(n.bit_length() - 1):
        x = x + exchange(x, axis, n, s)
    return x


def gathered_position(d, bits):
    return sum(((d >> s) & 1) << t for t, s in enumerate(bits))


def fanout_reduce_scatter(x, axis, n, bits):
    me = lax.axis_index(axis)
    rows = x.shape[0] // n
    own = lax.dynamic_slice_in_dim(x, gathered_position(me, bits) * rows, rows, axis=0)
    for k in range(1, n):
        block = lax.dynamic_slice_in_dim(x, gathered_position(me ^ k, bits) * rows, rows, axis=0)
        own = own + lax.ppermute(block, axis, [(a, a ^ k) for a in range(n)])
    return own


def gate_up(piece, w_gate, w_up, first_block, blocks, tile):
    rows, depth = piece.shape

    def kernel(x_ref, g_ref, u_ref, gate_ref, up_ref):
        x = x_ref[...]
        gate_ref[...] = jnp.dot(x, g_ref[...], preferred_element_type=jnp.float32)
        up_ref[...] = jnp.dot(x, u_ref[...], preferred_element_type=jnp.float32)

    weight_spec = pl.BlockSpec((depth, tile), lambda j: (0, first_block + j))
    out_spec = pl.BlockSpec((rows, tile), lambda j: (0, j))
    out = jax.ShapeDtypeStruct((rows, blocks * tile), jnp.float32)
    weight_bytes = 2 * depth * blocks * tile * w_gate.dtype.itemsize
    return pl.pallas_call(
        kernel,
        grid=(blocks,),
        in_specs=[pl.BlockSpec((rows, depth), lambda j: (0, 0)), weight_spec, weight_spec],
        out_specs=[out_spec, out_spec],
        out_shape=[out, out],
        cost_estimate=pl.CostEstimate(
            flops=4 * rows * depth * blocks * tile, transcendentals=0,
            bytes_accessed=weight_bytes + 8 * rows * blocks * tile),
        compiler_params=pltpu.CompilerParams(vmem_limit_bytes=8 * depth * tile * 2 + (4 << 20)),
    )(piece, w_gate, w_up)


def local(tokens, norm_gain, w_gate, w_up, w_down):
    ngx = lax.axis_size("gx")
    ngy = lax.axis_size("gy")
    features = tokens.shape[1] * ngy
    gx_levels = list(range(ngx.bit_length() - 1))
    if pairwise(ngx):
        raw = xor_all_gather(tokens, "gx", ngx, 0, gx_levels[::-1])
    else:
        raw = lax.all_gather(tokens, "gx", axis=0, tiled=True)
    values = raw.astype(jnp.float32)
    local_sq = jnp.sum(values * values, axis=1)
    if pairwise(ngy):
        total_sq = xor_all_reduce(local_sq, "gy", ngy)
    else:
        total_sq = lax.psum(local_sq, "gy")
    inverse = lax.rsqrt(total_sq / features + epsilon)
    piece = (values * inverse[:, None] * norm_gain[None, :]).astype(jnp.bfloat16)
    rows = piece.shape[0]

    width = w_gate.shape[1]
    chunks = CHUNKS if width % (CHUNKS * ngy * 128) == 0 else 1
    step = width // chunks
    gy_levels = list(range(ngy.bit_length() - 1))
    total = None
    anchor = None
    for c in range(chunks):
        cols = slice(c * step, (c + 1) * step)
        rows_in = piece
        if anchor is not None:
            rows_in, _ = lax.optimization_barrier((piece, anchor))
        if step % TILE == 0:
            gate_part, up_part = gate_up(rows_in, w_gate, w_up, c * step // TILE, step // TILE, TILE)
        else:
            gate_part = jnp.dot(rows_in, w_gate[:, cols], preferred_element_type=jnp.float32)
            up_part = jnp.dot(rows_in, w_up[:, cols], preferred_element_type=jnp.float32)
        if pairwise(ngy):
            first = xor_reduce_scatter([gate_part, up_part], "gy", ngy, 1, gy_levels[:1])
            anchor = first[0]
            gate, up = xor_reduce_scatter(first, "gy", ngy, 1, gy_levels[1:])
        else:
            gate = lax.psum_scatter(gate_part, "gy", scatter_dimension=1, tiled=True)
            up = lax.psum_scatter(up_part, "gy", scatter_dimension=1, tiled=True)
        hidden = (jax.nn.silu(gate) * up).astype(jnp.bfloat16)
        if pairwise(ngy):
            hidden_all = xor_all_gather(hidden, "gy", ngy, 1, gy_levels[::-1])
        else:
            hidden_all = lax.all_gather(hidden, "gy", axis=1, tiled=True)
        term = jnp.dot(hidden_all, w_down[cols, :], preferred_element_type=jnp.float32)
        total = term if total is None else total + term
    if pairwise(ngx):
        result = fanout_reduce_scatter(total, "gx", ngx, gx_levels[::-1])
    else:
        result = lax.psum_scatter(total, "gx", scatter_dimension=0, tiled=True)
    return result.astype(jnp.bfloat16)


def solution(mesh):
    in_specs = (P(("groups", "gx"), "gy"), P("gy"), P("gy", "gx"), P("gy", "gx"), P("gx", "gy"))
    out_specs = P(("groups", "gx"), "gy")
    return jax.shard_map(local, mesh=mesh, in_specs=in_specs, out_specs=out_specs, check_vma=False)
```

```python
import jax
import jax.numpy as jnp
from jax import lax
from jax.experimental import pallas as pl
from jax.experimental.pallas import tpu as pltpu
from jax.sharding import PartitionSpec as P


epsilon = 1e-06

EXCHANGE_MAX = 8
CHUNKS = 2
TILE = 768


def pairwise(n):
    return n <= EXCHANGE_MAX and n & (n - 1) == 0


def exchange(x, axis, n, s):
    return lax.ppermute(x, axis, [(a, a ^ (1 << s)) for a in range(n)])


def xor_reduce_scatter(parts, axis, n, dim, bits):
    me = lax.axis_index(axis)
    for s in bits:
        bit = (me >> s) & 1
        half = parts[0].shape[dim] // 2
        keep = [lax.dynamic_slice_in_dim(p, bit * half, half, axis=dim) for p in parts]
        send = [lax.dynamic_slice_in_dim(p, (1 - bit) * half, half, axis=dim) for p in parts]
        got = exchange(jnp.stack(send), axis, n, s)
        parts = [k + got[i] for i, k in enumerate(keep)]
    return parts


def xor_all_gather(x, axis, n, dim, bits):
    me = lax.axis_index(axis)
    for s in bits:
        other = exchange(x, axis, n, s)
        low = jnp.concatenate([x, other], axis=dim)
        high = jnp.concatenate([other, x], axis=dim)
        x = jnp.where(((me >> s) & 1) == 0, low, high)
    return x


def xor_all_reduce(x, axis, n):
    for s in range(n.bit_length() - 1):
        x = x + exchange(x, axis, n, s)
    return x


def gathered_position(d, bits):
    return sum(((d >> s) & 1) << t for t, s in enumerate(bits))


def fanout_reduce_scatter(x, axis, n, bits):
    me = lax.axis_index(axis)
    rows = x.shape[0] // n
    own = lax.dynamic_slice_in_dim(x, gathered_position(me, bits) * rows, rows, axis=0)
    for k in range(1, n):
        block = lax.dynamic_slice_in_dim(x, gathered_position(me ^ k, bits) * rows, rows, axis=0)
        own = own + lax.ppermute(block, axis, [(a, a ^ k) for a in range(n)])
    return own


def gate_up(piece, w_gate, w_up, first_block, blocks, tile):
    rows, depth = piece.shape

    def kernel(x_ref, g_ref, u_ref, gate_ref, up_ref):
        x = x_ref[...]
        gate_ref[...] = jnp.dot(x, g_ref[...], preferred_element_type=jnp.float32)
        up_ref[...] = jnp.dot(x, u_ref[...], preferred_element_type=jnp.float32)

    weight_spec = pl.BlockSpec((depth, tile), lambda j: (0, first_block + j))
    out_spec = pl.BlockSpec((rows, tile), lambda j: (0, j))
    out = jax.ShapeDtypeStruct((rows, blocks * tile), jnp.float32)
    weight_bytes = 2 * depth * blocks * tile * w_gate.dtype.itemsize
    return pl.pallas_call(
        kernel,
        grid=(blocks,),
        in_specs=[pl.BlockSpec((rows, depth), lambda j: (0, 0)), weight_spec, weight_spec],
        out_specs=[out_spec, out_spec],
        out_shape=[out, out],
        cost_estimate=pl.CostEstimate(
            flops=4 * rows * depth * blocks * tile, transcendentals=0,
            bytes_accessed=weight_bytes + 8 * rows * blocks * tile),
        compiler_params=pltpu.CompilerParams(vmem_limit_bytes=8 * depth * tile * 2 + (4 << 20)),
    )(piece, pltpu.with_memory_space_constraint(w_gate, pltpu.HBM),
      pltpu.with_memory_space_constraint(w_up, pltpu.HBM))


def local(tokens, norm_gain, w_gate, w_up, w_down):
    ngx = lax.axis_size("gx")
    ngy = lax.axis_size("gy")
    features = tokens.shape[1] * ngy
    gx_levels = list(range(ngx.bit_length() - 1))
    if pairwise(ngx):
        raw = xor_all_gather(tokens, "gx", ngx, 0, gx_levels[::-1])
    else:
        raw = lax.all_gather(tokens, "gx", axis=0, tiled=True)
    values = raw.astype(jnp.float32)
    local_sq = jnp.sum(values * values, axis=1)
    if pairwise(ngy):
        total_sq = xor_all_reduce(local_sq, "gy", ngy)
    else:
        total_sq = lax.psum(local_sq, "gy")
    inverse = lax.rsqrt(total_sq / features + epsilon)
    piece = (values * inverse[:, None] * norm_gain[None, :]).astype(jnp.bfloat16)
    rows = piece.shape[0]

    width = w_gate.shape[1]
    chunks = CHUNKS if width % (CHUNKS * ngy * 128) == 0 else 1
    step = width // chunks
    gy_levels = list(range(ngy.bit_length() - 1))
    total = None
    anchor = None
    for c in range(chunks):
        cols = slice(c * step, (c + 1) * step)
        rows_in = piece
        if anchor is not None:
            rows_in, _ = lax.optimization_barrier((piece, anchor))
        if step % TILE == 0:
            gate_part, up_part = gate_up(rows_in, w_gate, w_up, c * step // TILE, step // TILE, TILE)
        else:
            gate_part = jnp.dot(rows_in, w_gate[:, cols], preferred_element_type=jnp.float32)
            up_part = jnp.dot(rows_in, w_up[:, cols], preferred_element_type=jnp.float32)
        if pairwise(ngy):
            first = xor_reduce_scatter([gate_part, up_part], "gy", ngy, 1, gy_levels[:1])
            anchor = first[0]
            gate, up = xor_reduce_scatter(first, "gy", ngy, 1, gy_levels[1:])
        else:
            gate = lax.psum_scatter(gate_part, "gy", scatter_dimension=1, tiled=True)
            up = lax.psum_scatter(up_part, "gy", scatter_dimension=1, tiled=True)
        hidden = (jax.nn.silu(gate) * up).astype(jnp.bfloat16)
        if pairwise(ngy):
            hidden_all = xor_all_gather(hidden, "gy", ngy, 1, gy_levels[::-1])
        else:
            hidden_all = lax.all_gather(hidden, "gy", axis=1, tiled=True)
        term = jnp.dot(hidden_all, w_down[cols, :], preferred_element_type=jnp.float32)
        total = term if total is None else total + term
    if pairwise(ngx):
        result = fanout_reduce_scatter(total, "gx", ngx, gx_levels[::-1])
    else:
        result = lax.psum_scatter(total, "gx", scatter_dimension=0, tiled=True)
    return result.astype(jnp.bfloat16)


def solution(mesh):
    in_specs = (P(("groups", "gx"), "gy"), P("gy"), P("gy", "gx"), P("gy", "gx"), P("gx", "gy"))
    out_specs = P(("groups", "gx"), "gy")
    return jax.shard_map(local, mesh=mesh, in_specs=in_specs, out_specs=out_specs, check_vma=False)
```

```python
import jax
import jax.numpy as jnp
from jax import lax
from jax.sharding import PartitionSpec as P


epsilon = 1e-06

EXCHANGE_MAX = 8
CHUNKS = 2


def pairwise(n):
    return n <= EXCHANGE_MAX and n & (n - 1) == 0


def exchange(x, axis, n, s):
    return lax.ppermute(x, axis, [(a, a ^ (1 << s)) for a in range(n)])


def xor_reduce_scatter(parts, axis, n, dim, bits):
    me = lax.axis_index(axis)
    for s in bits:
        bit = (me >> s) & 1
        half = parts[0].shape[dim] // 2
        keep = [lax.dynamic_slice_in_dim(p, bit * half, half, axis=dim) for p in parts]
        send = [lax.dynamic_slice_in_dim(p, (1 - bit) * half, half, axis=dim) for p in parts]
        got = exchange(jnp.stack(send), axis, n, s)
        parts = [k + got[i] for i, k in enumerate(keep)]
    return parts


def xor_all_gather(x, axis, n, dim, bits):
    me = lax.axis_index(axis)
    for s in bits:
        other = exchange(x, axis, n, s)
        low = jnp.concatenate([x, other], axis=dim)
        high = jnp.concatenate([other, x], axis=dim)
        x = jnp.where(((me >> s) & 1) == 0, low, high)
    return x


def xor_all_reduce(x, axis, n):
    for s in range(n.bit_length() - 1):
        x = x + exchange(x, axis, n, s)
    return x


def gathered_position(d, bits):
    return sum(((d >> s) & 1) << t for t, s in enumerate(bits))


def fanout_reduce_scatter(x, axis, n, bits):
    me = lax.axis_index(axis)
    rows = x.shape[0] // n
    own = lax.dynamic_slice_in_dim(x, gathered_position(me, bits) * rows, rows, axis=0)
    for k in range(1, n):
        block = lax.dynamic_slice_in_dim(x, gathered_position(me ^ k, bits) * rows, rows, axis=0)
        own = own + lax.ppermute(block, axis, [(a, a ^ k) for a in range(n)])
    return own


def fanout_all_gather(x, axis, n, bits):
    me = lax.axis_index(axis)
    rows = x.shape[0]
    out = jnp.zeros((n * rows,) + x.shape[1:], x.dtype)
    for k in range(n):
        block = x if k == 0 else lax.ppermute(x, axis, [(a, a ^ k) for a in range(n)])
        out = lax.dynamic_update_slice_in_dim(out, block, gathered_position(me ^ k, bits) * rows, axis=0)
    return out


def fanout_all_reduce(x, axis, n):
    me = lax.axis_index(axis)
    got = jnp.stack([x] + [lax.ppermute(x, axis, [(a, a ^ k) for a in range(n)]) for k in range(1, n)])
    ordered = jnp.take(got, jnp.arange(n) ^ me, axis=0)
    return jnp.sum(ordered, axis=0)


def local(tokens, norm_gain, w_gate, w_up, w_down):
    ngx = lax.axis_size("gx")
    ngy = lax.axis_size("gy")
    features = tokens.shape[1] * ngy
    gx_levels = list(range(ngx.bit_length() - 1))
    if pairwise(ngx):
        raw = fanout_all_gather(tokens, "gx", ngx, gx_levels[::-1])
    else:
        raw = lax.all_gather(tokens, "gx", axis=0, tiled=True)
    values = raw.astype(jnp.float32)
    local_sq = jnp.sum(values * values, axis=1)
    if pairwise(ngy):
        total_sq = fanout_all_reduce(local_sq, "gy", ngy)
    else:
        total_sq = lax.psum(local_sq, "gy")
    inverse = lax.rsqrt(total_sq / features + epsilon)
    piece = (values * inverse[:, None] * norm_gain[None, :]).astype(jnp.bfloat16)
    rows = piece.shape[0]

    width = w_gate.shape[1]
    chunks = CHUNKS if width % (CHUNKS * ngy * 128) == 0 else 1
    step = width // chunks
    gy_levels = list(range(ngy.bit_length() - 1))
    total = None
    for c in range(chunks):
        cols = slice(c * step, (c + 1) * step)
        gate_part = jnp.dot(piece, w_gate[:, cols], preferred_element_type=jnp.float32)
        up_part = jnp.dot(piece, w_up[:, cols], preferred_element_type=jnp.float32)
        if pairwise(ngy):
            gate, up = xor_reduce_scatter([gate_part, up_part], "gy", ngy, 1, gy_levels)
        else:
            gate = lax.psum_scatter(gate_part, "gy", scatter_dimension=1, tiled=True)
            up = lax.psum_scatter(up_part, "gy", scatter_dimension=1, tiled=True)
        hidden = (jax.nn.silu(gate) * up).astype(jnp.bfloat16)
        if pairwise(ngy):
            hidden_all = xor_all_gather(hidden, "gy", ngy, 1, gy_levels[::-1])
        else:
            hidden_all = lax.all_gather(hidden, "gy", axis=1, tiled=True)
        term = jnp.dot(hidden_all, w_down[cols, :], preferred_element_type=jnp.float32)
        total = term if total is None else total + term
    if pairwise(ngx):
        result = fanout_reduce_scatter(total, "gx", ngx, gx_levels[::-1])
    else:
        result = lax.psum_scatter(total, "gx", scatter_dimension=0, tiled=True)
    return result.astype(jnp.bfloat16)


def solution(mesh):
    in_specs = (P(("groups", "gx"), "gy"), P("gy"), P("gy", "gx"), P("gy", "gx"), P("gx", "gy"))
    out_specs = P(("groups", "gx"), "gy")
    return jax.shard_map(local, mesh=mesh, in_specs=in_specs, out_specs=out_specs, check_vma=False)
```

```python
import jax
import jax.numpy as jnp
from jax import lax
from jax.experimental import pallas as pl
from jax.experimental.pallas import tpu as pltpu
from jax.sharding import PartitionSpec as P


epsilon = 1e-06

EXCHANGE_MAX = 8
CHUNKS = 2


def pairwise(n):
    return n <= EXCHANGE_MAX and n & (n - 1) == 0


def exchange(x, axis, n, s):
    return lax.ppermute(x, axis, [(a, a ^ (1 << s)) for a in range(n)])


def xor_reduce_scatter(parts, axis, n, dim, bits):
    me = lax.axis_index(axis)
    for s in bits:
        bit = (me >> s) & 1
        half = parts[0].shape[dim] // 2
        keep = [lax.dynamic_slice_in_dim(p, bit * half, half, axis=dim) for p in parts]
        send = [lax.dynamic_slice_in_dim(p, (1 - bit) * half, half, axis=dim) for p in parts]
        got = exchange(jnp.stack(send), axis, n, s)
        parts = [k + got[i] for i, k in enumerate(keep)]
    return parts


def xor_all_gather(x, axis, n, dim, bits):
    me = lax.axis_index(axis)
    for s in bits:
        other = exchange(x, axis, n, s)
        low = jnp.concatenate([x, other], axis=dim)
        high = jnp.concatenate([other, x], axis=dim)
        x = jnp.where(((me >> s) & 1) == 0, low, high)
    return x


def xor_all_reduce(x, axis, n):
    for s in range(n.bit_length() - 1):
        x = x + exchange(x, axis, n, s)
    return x


def gathered_position(d, bits):
    return sum(((d >> s) & 1) << t for t, s in enumerate(bits))


def fanout_reduce_scatter(x, axis, n, bits):
    me = lax.axis_index(axis)
    rows = x.shape[0] // n
    own = lax.dynamic_slice_in_dim(x, gathered_position(me, bits) * rows, rows, axis=0)
    for k in range(1, n):
        block = lax.dynamic_slice_in_dim(x, gathered_position(me ^ k, bits) * rows, rows, axis=0)
        own = own + lax.ppermute(block, axis, [(a, a ^ k) for a in range(n)])
    return own


def fanout_all_gather(x, axis, n, bits):
    me = lax.axis_index(axis)
    rows = x.shape[0]
    out = jnp.zeros((n * rows,) + x.shape[1:], x.dtype)
    for k in range(n):
        block = x if k == 0 else lax.ppermute(x, axis, [(a, a ^ k) for a in range(n)])
        out = lax.dynamic_update_slice_in_dim(out, block, gathered_position(me ^ k, bits) * rows, axis=0)
    return out


def fanout_all_reduce(x, axis, n):
    me = lax.axis_index(axis)
    got = jnp.stack([x] + [lax.ppermute(x, axis, [(a, a ^ k) for a in range(n)]) for k in range(1, n)])
    ordered = jnp.take(got, jnp.arange(n) ^ me, axis=0)
    return jnp.sum(ordered, axis=0)


def rows_to_vmem(w, start, count):
    size = count * w.shape[1] * w.dtype.itemsize

    def kernel(src, dst, sem):
        copy = pltpu.make_async_copy(src.at[pl.ds(start, count), :], dst, sem)
        copy.start()
        copy.wait()

    return pl.pallas_call(
        kernel,
        out_shape=jax.ShapeDtypeStruct((count, w.shape[1]), w.dtype),
        in_specs=[pl.BlockSpec(memory_space=pl.ANY)],
        out_specs=pl.BlockSpec(memory_space=pltpu.VMEM),
        scratch_shapes=[pltpu.SemaphoreType.DMA(())],
        cost_estimate=pl.CostEstimate(flops=0, transcendentals=0, bytes_accessed=2 * size),
        compiler_params=pltpu.CompilerParams(vmem_limit_bytes=size + (2 << 20)),
    )(pltpu.with_memory_space_constraint(w, pltpu.HBM))


def local(tokens, norm_gain, w_gate, w_up, w_down):
    ngx = lax.axis_size("gx")
    ngy = lax.axis_size("gy")
    features = tokens.shape[1] * ngy
    gx_levels = list(range(ngx.bit_length() - 1))
    if pairwise(ngx):
        raw = fanout_all_gather(tokens, "gx", ngx, gx_levels[::-1])
    else:
        raw = lax.all_gather(tokens, "gx", axis=0, tiled=True)
    values = raw.astype(jnp.float32)
    local_sq = jnp.sum(values * values, axis=1)
    if pairwise(ngy):
        total_sq = fanout_all_reduce(local_sq, "gy", ngy)
    else:
        total_sq = lax.psum(local_sq, "gy")
    inverse = lax.rsqrt(total_sq / features + epsilon)
    piece = (values * inverse[:, None] * norm_gain[None, :]).astype(jnp.bfloat16)
    rows = piece.shape[0]

    width = w_gate.shape[1]
    chunks = CHUNKS if width % (CHUNKS * ngy * 128) == 0 else 1
    step = width // chunks
    gy_levels = list(range(ngy.bit_length() - 1))
    total = None
    for c in range(chunks):
        cols = slice(c * step, (c + 1) * step)
        gate_part = jnp.dot(piece, w_gate[:, cols], preferred_element_type=jnp.float32)
        up_part = jnp.dot(piece, w_up[:, cols], preferred_element_type=jnp.float32)
        if pairwise(ngy):
            first = xor_reduce_scatter([gate_part, up_part], "gy", ngy, 1, gy_levels[:1])
            if c == 0:
                source, _ = lax.optimization_barrier((w_down, first[0]))
                staged = [rows_to_vmem(source, k * step, step) for k in range(chunks)]
            gate, up = xor_reduce_scatter(first, "gy", ngy, 1, gy_levels[1:])
        else:
            gate = lax.psum_scatter(gate_part, "gy", scatter_dimension=1, tiled=True)
            up = lax.psum_scatter(up_part, "gy", scatter_dimension=1, tiled=True)
        hidden = (jax.nn.silu(gate) * up).astype(jnp.bfloat16)
        if pairwise(ngy):
            hidden_all = xor_all_gather(hidden, "gy", ngy, 1, gy_levels[::-1])
        else:
            hidden_all = lax.all_gather(hidden, "gy", axis=1, tiled=True)
        down = staged[c] if pairwise(ngy) else w_down[cols, :]
        term = jnp.dot(hidden_all, down, preferred_element_type=jnp.float32)
        total = term if total is None else total + term
    if pairwise(ngx):
        result = fanout_reduce_scatter(total, "gx", ngx, gx_levels[::-1])
    else:
        result = lax.psum_scatter(total, "gx", scatter_dimension=0, tiled=True)
    return result.astype(jnp.bfloat16)


def solution(mesh):
    in_specs = (P(("groups", "gx"), "gy"), P("gy"), P("gy", "gx"), P("gy", "gx"), P("gx", "gy"))
    out_specs = P(("groups", "gx"), "gy")
    return jax.shard_map(local, mesh=mesh, in_specs=in_specs, out_specs=out_specs, check_vma=False)
```

```python
import jax
import jax.numpy as jnp
from jax import lax
from jax.experimental import pallas as pl
from jax.experimental.pallas import tpu as pltpu
from jax.sharding import PartitionSpec as P


epsilon = 1e-06

EXCHANGE_MAX = 8
CHUNKS = 2


def pairwise(n):
    return n <= EXCHANGE_MAX and n & (n - 1) == 0


def exchange(x, axis, n, s):
    return lax.ppermute(x, axis, [(a, a ^ (1 << s)) for a in range(n)])


def xor_reduce_scatter(parts, axis, n, dim, bits):
    me = lax.axis_index(axis)
    for s in bits:
        bit = (me >> s) & 1
        half = parts[0].shape[dim] // 2
        keep = [lax.dynamic_slice_in_dim(p, bit * half, half, axis=dim) for p in parts]
        send = [lax.dynamic_slice_in_dim(p, (1 - bit) * half, half, axis=dim) for p in parts]
        got = exchange(jnp.stack(send), axis, n, s)
        parts = [k + got[i] for i, k in enumerate(keep)]
    return parts


def xor_all_gather(x, axis, n, dim, bits):
    me = lax.axis_index(axis)
    for s in bits:
        other = exchange(x, axis, n, s)
        low = jnp.concatenate([x, other], axis=dim)
        high = jnp.concatenate([other, x], axis=dim)
        x = jnp.where(((me >> s) & 1) == 0, low, high)
    return x


def xor_all_reduce(x, axis, n):
    for s in range(n.bit_length() - 1):
        x = x + exchange(x, axis, n, s)
    return x


def gathered_position(d, bits):
    return sum(((d >> s) & 1) << t for t, s in enumerate(bits))


def fanout_reduce_scatter(x, axis, n, bits):
    me = lax.axis_index(axis)
    rows = x.shape[0] // n
    own = lax.dynamic_slice_in_dim(x, gathered_position(me, bits) * rows, rows, axis=0)
    for k in range(1, n):
        block = lax.dynamic_slice_in_dim(x, gathered_position(me ^ k, bits) * rows, rows, axis=0)
        own = own + lax.ppermute(block, axis, [(a, a ^ k) for a in range(n)])
    return own


def fanout_all_gather(x, axis, n, bits):
    me = lax.axis_index(axis)
    rows = x.shape[0]
    out = jnp.zeros((n * rows,) + x.shape[1:], x.dtype)
    for k in range(n):
        block = x if k == 0 else lax.ppermute(x, axis, [(a, a ^ k) for a in range(n)])
        out = lax.dynamic_update_slice_in_dim(out, block, gathered_position(me ^ k, bits) * rows, axis=0)
    return out


def fanout_all_reduce(x, axis, n):
    me = lax.axis_index(axis)
    got = jnp.stack([x] + [lax.ppermute(x, axis, [(a, a ^ k) for a in range(n)]) for k in range(1, n)])
    ordered = jnp.take(got, jnp.arange(n) ^ me, axis=0)
    return jnp.sum(ordered, axis=0)


def rows_to_vmem(w, start, count):
    size = count * w.shape[1] * w.dtype.itemsize

    def kernel(src, dst, sem):
        copy = pltpu.make_async_copy(src.at[pl.ds(start, count), :], dst, sem)
        copy.start()
        copy.wait()

    return pl.pallas_call(
        kernel,
        out_shape=jax.ShapeDtypeStruct((count, w.shape[1]), w.dtype),
        in_specs=[pl.BlockSpec(memory_space=pl.ANY)],
        out_specs=pl.BlockSpec(memory_space=pltpu.VMEM),
        scratch_shapes=[pltpu.SemaphoreType.DMA(())],
        cost_estimate=pl.CostEstimate(flops=0, transcendentals=0, bytes_accessed=2 * size),
        compiler_params=pltpu.CompilerParams(vmem_limit_bytes=size + (2 << 20)),
    )(pltpu.with_memory_space_constraint(w, pltpu.HBM))


def local(tokens, norm_gain, w_gate, w_up, w_down):
    ngx = lax.axis_size("gx")
    ngy = lax.axis_size("gy")
    features = tokens.shape[1] * ngy
    gx_levels = list(range(ngx.bit_length() - 1))
    if pairwise(ngx):
        raw = fanout_all_gather(tokens, "gx", ngx, gx_levels[::-1])
    else:
        raw = lax.all_gather(tokens, "gx", axis=0, tiled=True)
    values = raw.astype(jnp.float32)
    local_sq = jnp.sum(values * values, axis=1)
    if pairwise(ngy):
        total_sq = fanout_all_reduce(local_sq, "gy", ngy)
    else:
        total_sq = lax.psum(local_sq, "gy")
    inverse = lax.rsqrt(total_sq / features + epsilon)
    piece = (values * inverse[:, None] * norm_gain[None, :]).astype(jnp.bfloat16)
    rows = piece.shape[0]

    width = w_gate.shape[1]
    chunks = CHUNKS if width % (CHUNKS * ngy * 128) == 0 else 1
    step = width // chunks
    gy_levels = list(range(ngy.bit_length() - 1))
    total = None
    for c in range(chunks):
        cols = slice(c * step, (c + 1) * step)
        gate_part = jnp.dot(piece, w_gate[:, cols], preferred_element_type=jnp.float32)
        up_part = jnp.dot(piece, w_up[:, cols], preferred_element_type=jnp.float32)
        if pairwise(ngy):
            first = xor_reduce_scatter([gate_part, up_part], "gy", ngy, 1, gy_levels[:1])
            if c == 0:
                source, _ = lax.optimization_barrier((w_down, first[0]))
                staged = [rows_to_vmem(source, 0, step)]
            gate, up = xor_reduce_scatter(first, "gy", ngy, 1, gy_levels[1:])
            if c == 0:
                for k in range(1, chunks):
                    source, _ = lax.optimization_barrier((w_down, gate))
                    staged.append(rows_to_vmem(source, k * step, step))
        else:
            gate = lax.psum_scatter(gate_part, "gy", scatter_dimension=1, tiled=True)
            up = lax.psum_scatter(up_part, "gy", scatter_dimension=1, tiled=True)
        hidden = (jax.nn.silu(gate) * up).astype(jnp.bfloat16)
        if pairwise(ngy):
            hidden_all = xor_all_gather(hidden, "gy", ngy, 1, gy_levels[::-1])
        else:
            hidden_all = lax.all_gather(hidden, "gy", axis=1, tiled=True)
        down = staged[c] if pairwise(ngy) else w_down[cols, :]
        term = jnp.dot(hidden_all, down, preferred_element_type=jnp.float32)
        total = term if total is None else total + term
    if pairwise(ngx):
        result = fanout_reduce_scatter(total, "gx", ngx, gx_levels[::-1])
    else:
        result = lax.psum_scatter(total, "gx", scatter_dimension=0, tiled=True)
    return result.astype(jnp.bfloat16)


def solution(mesh):
    in_specs = (P(("groups", "gx"), "gy"), P("gy"), P("gy", "gx"), P("gy", "gx"), P("gx", "gy"))
    out_specs = P(("groups", "gx"), "gy")
    return jax.shard_map(local, mesh=mesh, in_specs=in_specs, out_specs=out_specs, check_vma=False)
```

```python
import jax
import jax.numpy as jnp
from jax import lax
from jax.experimental import pallas as pl
from jax.experimental.pallas import tpu as pltpu
from jax.sharding import PartitionSpec as P


epsilon = 1e-06

EXCHANGE_MAX = 8
CHUNKS = 2
STREAMS = 4


def pairwise(n):
    return n <= EXCHANGE_MAX and n & (n - 1) == 0


def exchange(x, axis, n, s):
    return lax.ppermute(x, axis, [(a, a ^ (1 << s)) for a in range(n)])


def xor_reduce_scatter(parts, axis, n, dim, bits):
    me = lax.axis_index(axis)
    for s in bits:
        bit = (me >> s) & 1
        half = parts[0].shape[dim] // 2
        keep = [lax.dynamic_slice_in_dim(p, bit * half, half, axis=dim) for p in parts]
        send = [lax.dynamic_slice_in_dim(p, (1 - bit) * half, half, axis=dim) for p in parts]
        got = exchange(jnp.stack(send), axis, n, s)
        parts = [k + got[i] for i, k in enumerate(keep)]
    return parts


def xor_all_gather(x, axis, n, dim, bits):
    me = lax.axis_index(axis)
    for s in bits:
        other = exchange(x, axis, n, s)
        low = jnp.concatenate([x, other], axis=dim)
        high = jnp.concatenate([other, x], axis=dim)
        x = jnp.where(((me >> s) & 1) == 0, low, high)
    return x


def xor_all_reduce(x, axis, n):
    for s in range(n.bit_length() - 1):
        x = x + exchange(x, axis, n, s)
    return x


def gathered_position(d, bits):
    return sum(((d >> s) & 1) << t for t, s in enumerate(bits))


def fanout_reduce_scatter(x, axis, n, bits):
    me = lax.axis_index(axis)
    rows = x.shape[0] // n
    own = lax.dynamic_slice_in_dim(x, gathered_position(me, bits) * rows, rows, axis=0)
    for k in range(1, n):
        block = lax.dynamic_slice_in_dim(x, gathered_position(me ^ k, bits) * rows, rows, axis=0)
        own = own + lax.ppermute(block, axis, [(a, a ^ k) for a in range(n)])
    return own


def fanout_all_gather(x, axis, n, bits):
    me = lax.axis_index(axis)
    rows = x.shape[0]
    out = jnp.zeros((n * rows,) + x.shape[1:], x.dtype)
    for k in range(n):
        block = x if k == 0 else lax.ppermute(x, axis, [(a, a ^ k) for a in range(n)])
        out = lax.dynamic_update_slice_in_dim(out, block, gathered_position(me ^ k, bits) * rows, axis=0)
    return out


def fanout_all_reduce(x, axis, n):
    me = lax.axis_index(axis)
    got = jnp.stack([x] + [lax.ppermute(x, axis, [(a, a ^ k) for a in range(n)]) for k in range(1, n)])
    ordered = jnp.take(got, jnp.arange(n) ^ me, axis=0)
    return jnp.sum(ordered, axis=0)


def rows_to_vmem(w, start, count):
    size = count * w.shape[1] * w.dtype.itemsize

    def kernel(src, dst, sem):
        streams = STREAMS if count % (STREAMS * 16) == 0 else 1
        part = count // streams
        copies = [
            pltpu.make_async_copy(
                src.at[pl.ds(start + i * part, part), :], dst.at[pl.ds(i * part, part), :], sem.at[i])
            for i in range(streams)
        ]
        for copy in copies:
            copy.start()
        for copy in copies:
            copy.wait()

    return pl.pallas_call(
        kernel,
        out_shape=jax.ShapeDtypeStruct((count, w.shape[1]), w.dtype),
        in_specs=[pl.BlockSpec(memory_space=pl.ANY)],
        out_specs=pl.BlockSpec(memory_space=pltpu.VMEM),
        scratch_shapes=[pltpu.SemaphoreType.DMA((STREAMS,))],
        cost_estimate=pl.CostEstimate(flops=0, transcendentals=0, bytes_accessed=2 * size),
        compiler_params=pltpu.CompilerParams(vmem_limit_bytes=size + (2 << 20)),
    )(pltpu.with_memory_space_constraint(w, pltpu.HBM))


def local(tokens, norm_gain, w_gate, w_up, w_down):
    ngx = lax.axis_size("gx")
    ngy = lax.axis_size("gy")
    features = tokens.shape[1] * ngy
    gx_levels = list(range(ngx.bit_length() - 1))
    if pairwise(ngx):
        raw = fanout_all_gather(tokens, "gx", ngx, gx_levels[::-1])
    else:
        raw = lax.all_gather(tokens, "gx", axis=0, tiled=True)
    values = raw.astype(jnp.float32)
    local_sq = jnp.sum(values * values, axis=1)
    if pairwise(ngy):
        total_sq = fanout_all_reduce(local_sq, "gy", ngy)
    else:
        total_sq = lax.psum(local_sq, "gy")
    inverse = lax.rsqrt(total_sq / features + epsilon)
    piece = (values * inverse[:, None] * norm_gain[None, :]).astype(jnp.bfloat16)
    rows = piece.shape[0]

    width = w_gate.shape[1]
    chunks = CHUNKS if width % (CHUNKS * ngy * 128) == 0 else 1
    step = width // chunks
    gy_levels = list(range(ngy.bit_length() - 1))
    total = None
    for c in range(chunks):
        cols = slice(c * step, (c + 1) * step)
        gate_part = jnp.dot(piece, w_gate[:, cols], preferred_element_type=jnp.float32)
        up_part = jnp.dot(piece, w_up[:, cols], preferred_element_type=jnp.float32)
        if pairwise(ngy):
            first = xor_reduce_scatter([gate_part, up_part], "gy", ngy, 1, gy_levels[:1])
            if c == 0:
                source, _ = lax.optimization_barrier((w_down, first[0]))
                staged = [rows_to_vmem(source, 0, step)]
            gate, up = xor_reduce_scatter(first, "gy", ngy, 1, gy_levels[1:])
            if c == 0:
                for k in range(1, chunks):
                    source, _ = lax.optimization_barrier((w_down, gate))
                    staged.append(rows_to_vmem(source, k * step, step))
        else:
            gate = lax.psum_scatter(gate_part, "gy", scatter_dimension=1, tiled=True)
            up = lax.psum_scatter(up_part, "gy", scatter_dimension=1, tiled=True)
        hidden = (jax.nn.silu(gate) * up).astype(jnp.bfloat16)
        if pairwise(ngy):
            hidden_all = xor_all_gather(hidden, "gy", ngy, 1, gy_levels[::-1])
        else:
            hidden_all = lax.all_gather(hidden, "gy", axis=1, tiled=True)
        down = staged[c] if pairwise(ngy) else w_down[cols, :]
        term = jnp.dot(hidden_all, down, preferred_element_type=jnp.float32)
        total = term if total is None else total + term
    if pairwise(ngx):
        result = fanout_reduce_scatter(total, "gx", ngx, gx_levels[::-1])
    else:
        result = lax.psum_scatter(total, "gx", scatter_dimension=0, tiled=True)
    return result.astype(jnp.bfloat16)


def solution(mesh):
    in_specs = (P(("groups", "gx"), "gy"), P("gy"), P("gy", "gx"), P("gy", "gx"), P("gx", "gy"))
    out_specs = P(("groups", "gx"), "gy")
    return jax.shard_map(local, mesh=mesh, in_specs=in_specs, out_specs=out_specs, check_vma=False)
```

```python
import jax
import jax.numpy as jnp
from jax import lax
from jax.experimental import pallas as pl
from jax.experimental.pallas import tpu as pltpu
from jax.sharding import PartitionSpec as P


epsilon = 1e-06

EXCHANGE_MAX = 8
CHUNKS = 1


def pairwise(n):
    return n <= EXCHANGE_MAX and n & (n - 1) == 0


def exchange(x, axis, n, s):
    return lax.ppermute(x, axis, [(a, a ^ (1 << s)) for a in range(n)])


def xor_reduce_scatter(parts, axis, n, dim, bits):
    me = lax.axis_index(axis)
    for s in bits:
        bit = (me >> s) & 1
        half = parts[0].shape[dim] // 2
        keep = [lax.dynamic_slice_in_dim(p, bit * half, half, axis=dim) for p in parts]
        send = [lax.dynamic_slice_in_dim(p, (1 - bit) * half, half, axis=dim) for p in parts]
        got = exchange(jnp.stack(send), axis, n, s)
        parts = [k + got[i] for i, k in enumerate(keep)]
    return parts


def xor_all_gather(x, axis, n, dim, bits):
    me = lax.axis_index(axis)
    for s in bits:
        other = exchange(x, axis, n, s)
        low = jnp.concatenate([x, other], axis=dim)
        high = jnp.concatenate([other, x], axis=dim)
        x = jnp.where(((me >> s) & 1) == 0, low, high)
    return x


def xor_all_reduce(x, axis, n):
    for s in range(n.bit_length() - 1):
        x = x + exchange(x, axis, n, s)
    return x


def gathered_position(d, bits):
    return sum(((d >> s) & 1) << t for t, s in enumerate(bits))


def fanout_reduce_scatter(x, axis, n, bits):
    me = lax.axis_index(axis)
    rows = x.shape[0] // n
    own = lax.dynamic_slice_in_dim(x, gathered_position(me, bits) * rows, rows, axis=0)
    for k in range(1, n):
        block = lax.dynamic_slice_in_dim(x, gathered_position(me ^ k, bits) * rows, rows, axis=0)
        own = own + lax.ppermute(block, axis, [(a, a ^ k) for a in range(n)])
    return own


def fanout_all_gather(x, axis, n, bits):
    me = lax.axis_index(axis)
    rows = x.shape[0]
    out = jnp.zeros((n * rows,) + x.shape[1:], x.dtype)
    for k in range(n):
        block = x if k == 0 else lax.ppermute(x, axis, [(a, a ^ k) for a in range(n)])
        out = lax.dynamic_update_slice_in_dim(out, block, gathered_position(me ^ k, bits) * rows, axis=0)
    return out


def fanout_all_reduce(x, axis, n):
    me = lax.axis_index(axis)
    got = jnp.stack([x] + [lax.ppermute(x, axis, [(a, a ^ k) for a in range(n)]) for k in range(1, n)])
    ordered = jnp.take(got, jnp.arange(n) ^ me, axis=0)
    return jnp.sum(ordered, axis=0)


def rows_to_vmem(w, start, count):
    size = count * w.shape[1] * w.dtype.itemsize

    def kernel(src, dst, sem):
        copy = pltpu.make_async_copy(src.at[pl.ds(start, count), :], dst, sem)
        copy.start()
        copy.wait()

    return pl.pallas_call(
        kernel,
        out_shape=jax.ShapeDtypeStruct((count, w.shape[1]), w.dtype),
        in_specs=[pl.BlockSpec(memory_space=pl.ANY)],
        out_specs=pl.BlockSpec(memory_space=pltpu.VMEM),
        scratch_shapes=[pltpu.SemaphoreType.DMA(())],
        cost_estimate=pl.CostEstimate(flops=0, transcendentals=0, bytes_accessed=2 * size),
        compiler_params=pltpu.CompilerParams(vmem_limit_bytes=size + (2 << 20)),
    )(pltpu.with_memory_space_constraint(w, pltpu.HBM))


def local(tokens, norm_gain, w_gate, w_up, w_down):
    ngx = lax.axis_size("gx")
    ngy = lax.axis_size("gy")
    features = tokens.shape[1] * ngy
    gx_levels = list(range(ngx.bit_length() - 1))
    if pairwise(ngx):
        raw = fanout_all_gather(tokens, "gx", ngx, gx_levels[::-1])
    else:
        raw = lax.all_gather(tokens, "gx", axis=0, tiled=True)
    values = raw.astype(jnp.float32)
    local_sq = jnp.sum(values * values, axis=1)
    if pairwise(ngy):
        total_sq = fanout_all_reduce(local_sq, "gy", ngy)
    else:
        total_sq = lax.psum(local_sq, "gy")
    inverse = lax.rsqrt(total_sq / features + epsilon)
    piece = (values * inverse[:, None] * norm_gain[None, :]).astype(jnp.bfloat16)
    rows = piece.shape[0]

    width = w_gate.shape[1]
    chunks = CHUNKS if width % (CHUNKS * ngy * 128) == 0 else 1
    step = width // chunks
    gy_levels = list(range(ngy.bit_length() - 1))
    total = None
    half = w_down.shape[0] // 2
    staged = None
    for c in range(chunks):
        cols = slice(c * step, (c + 1) * step)
        gate_part = jnp.dot(piece, w_gate[:, cols], preferred_element_type=jnp.float32)
        up_part = jnp.dot(piece, w_up[:, cols], preferred_element_type=jnp.float32)
        if pairwise(ngy):
            first = xor_reduce_scatter([gate_part, up_part], "gy", ngy, 1, gy_levels[:1])
            if c == 0:
                source, _ = lax.optimization_barrier((w_down, first[0]))
                staged = [rows_to_vmem(source, 0, half)]
            gate, up = xor_reduce_scatter(first, "gy", ngy, 1, gy_levels[1:])
            if c == 0:
                source, _ = lax.optimization_barrier((w_down, gate))
                staged.append(rows_to_vmem(source, half, half))
        else:
            gate = lax.psum_scatter(gate_part, "gy", scatter_dimension=1, tiled=True)
            up = lax.psum_scatter(up_part, "gy", scatter_dimension=1, tiled=True)
        hidden = (jax.nn.silu(gate) * up).astype(jnp.bfloat16)
        if pairwise(ngy):
            hidden_all = xor_all_gather(hidden, "gy", ngy, 1, gy_levels[::-1])
        else:
            hidden_all = lax.all_gather(hidden, "gy", axis=1, tiled=True)
        for p in range(2):
            lo, hi = max(c * step, p * half), min((c + 1) * step, (p + 1) * half)
            if lo >= hi:
                continue
            if staged is None:
                down = w_down[lo:hi, :]
            else:
                down = staged[p] if (lo, hi) == (p * half, (p + 1) * half) else staged[p][lo - p * half:hi - p * half]
            h = hidden_all if (lo, hi) == (c * step, (c + 1) * step) else hidden_all[:, lo - c * step:hi - c * step]
            term = jnp.dot(h, down, preferred_element_type=jnp.float32)
            total = term if total is None else total + term
    if pairwise(ngx):
        result = fanout_reduce_scatter(total, "gx", ngx, gx_levels[::-1])
    else:
        result = lax.psum_scatter(total, "gx", scatter_dimension=0, tiled=True)
    return result.astype(jnp.bfloat16)


def solution(mesh):
    in_specs = (P(("groups", "gx"), "gy"), P("gy"), P("gy", "gx"), P("gy", "gx"), P("gx", "gy"))
    out_specs = P(("groups", "gx"), "gy")
    return jax.shard_map(local, mesh=mesh, in_specs=in_specs, out_specs=out_specs, check_vma=False)
```

```python
import jax
import jax.numpy as jnp
from jax import lax
from jax.experimental import pallas as pl
from jax.experimental.pallas import tpu as pltpu
from jax.sharding import PartitionSpec as P


epsilon = 1e-06

EXCHANGE_MAX = 8
CHUNKS = 2


def pairwise(n):
    return n <= EXCHANGE_MAX and n & (n - 1) == 0


def exchange(x, axis, n, s):
    return lax.ppermute(x, axis, [(a, a ^ (1 << s)) for a in range(n)])


def xor_reduce_scatter(parts, axis, n, dim, bits):
    me = lax.axis_index(axis)
    for s in bits:
        bit = (me >> s) & 1
        half = parts[0].shape[dim] // 2
        keep = [lax.dynamic_slice_in_dim(p, bit * half, half, axis=dim) for p in parts]
        send = [lax.dynamic_slice_in_dim(p, (1 - bit) * half, half, axis=dim) for p in parts]
        got = exchange(jnp.stack(send), axis, n, s)
        parts = [k + got[i] for i, k in enumerate(keep)]
    return parts


def xor_all_gather(x, axis, n, dim, bits):
    me = lax.axis_index(axis)
    for s in bits:
        other = exchange(x, axis, n, s)
        low = jnp.concatenate([x, other], axis=dim)
        high = jnp.concatenate([other, x], axis=dim)
        x = jnp.where(((me >> s) & 1) == 0, low, high)
    return x


def xor_all_reduce(x, axis, n):
    for s in range(n.bit_length() - 1):
        x = x + exchange(x, axis, n, s)
    return x


def gathered_position(d, bits):
    return sum(((d >> s) & 1) << t for t, s in enumerate(bits))


def fanout_reduce_scatter(x, axis, n, bits):
    me = lax.axis_index(axis)
    rows = x.shape[0] // n
    own = lax.dynamic_slice_in_dim(x, gathered_position(me, bits) * rows, rows, axis=0)
    for k in range(1, n):
        block = lax.dynamic_slice_in_dim(x, gathered_position(me ^ k, bits) * rows, rows, axis=0)
        own = own + lax.ppermute(block, axis, [(a, a ^ k) for a in range(n)])
    return own


def fanout_all_gather(x, axis, n, bits):
    me = lax.axis_index(axis)
    rows = x.shape[0]
    out = jnp.zeros((n * rows,) + x.shape[1:], x.dtype)
    for k in range(n):
        block = x if k == 0 else lax.ppermute(x, axis, [(a, a ^ k) for a in range(n)])
        out = lax.dynamic_update_slice_in_dim(out, block, gathered_position(me ^ k, bits) * rows, axis=0)
    return out


def fanout_all_reduce(x, axis, n):
    me = lax.axis_index(axis)
    got = jnp.stack([x] + [lax.ppermute(x, axis, [(a, a ^ k) for a in range(n)]) for k in range(1, n)])
    ordered = jnp.take(got, jnp.arange(n) ^ me, axis=0)
    return jnp.sum(ordered, axis=0)


def rows_to_vmem(w, start, count):
    size = count * w.shape[1] * w.dtype.itemsize

    def kernel(src, dst, sem):
        copy = pltpu.make_async_copy(src.at[pl.ds(start, count), :], dst, sem)
        copy.start()
        copy.wait()

    return pl.pallas_call(
        kernel,
        out_shape=jax.ShapeDtypeStruct((count, w.shape[1]), w.dtype),
        in_specs=[pl.BlockSpec(memory_space=pl.ANY)],
        out_specs=pl.BlockSpec(memory_space=pltpu.VMEM),
        scratch_shapes=[pltpu.SemaphoreType.DMA(())],
        cost_estimate=pl.CostEstimate(flops=0, transcendentals=0, bytes_accessed=2 * size),
        compiler_params=pltpu.CompilerParams(vmem_limit_bytes=size + (2 << 20)),
    )(pltpu.with_memory_space_constraint(w, pltpu.HBM))


def relative_all_gather(x, axis, n):
    parts = [x] + [lax.ppermute(x, axis, [(a, a ^ k) for a in range(n)]) for k in range(1, n)]
    return jnp.concatenate(parts, axis=0)


def relative_reduce_scatter(x, axis, n):
    rows = x.shape[0] // n
    own = x[:rows]
    for k in range(1, n):
        block = x[k * rows:(k + 1) * rows]
        own = own + lax.ppermute(block, axis, [(a, a ^ k) for a in range(n)])
    return own


def local(tokens, norm_gain, w_gate, w_up, w_down):
    ngx = lax.axis_size("gx")
    ngy = lax.axis_size("gy")
    features = tokens.shape[1] * ngy
    gx_levels = list(range(ngx.bit_length() - 1))
    if pairwise(ngx):
        raw = relative_all_gather(tokens, "gx", ngx)
    else:
        raw = lax.all_gather(tokens, "gx", axis=0, tiled=True)
    values = raw.astype(jnp.float32)
    local_sq = jnp.sum(values * values, axis=1)
    if pairwise(ngy):
        total_sq = fanout_all_reduce(local_sq, "gy", ngy)
    else:
        total_sq = lax.psum(local_sq, "gy")
    inverse = lax.rsqrt(total_sq / features + epsilon)
    piece = (values * inverse[:, None] * norm_gain[None, :]).astype(jnp.bfloat16)
    rows = piece.shape[0]

    width = w_gate.shape[1]
    chunks = CHUNKS if width % (CHUNKS * ngy * 128) == 0 else 1
    step = width // chunks
    gy_levels = list(range(ngy.bit_length() - 1))
    total = None
    for c in range(chunks):
        cols = slice(c * step, (c + 1) * step)
        gate_part = jnp.dot(piece, w_gate[:, cols], preferred_element_type=jnp.float32)
        up_part = jnp.dot(piece, w_up[:, cols], preferred_element_type=jnp.float32)
        if pairwise(ngy):
            first = xor_reduce_scatter([gate_part, up_part], "gy", ngy, 1, gy_levels[:1])
            if c == 0:
                source, _ = lax.optimization_barrier((w_down, first[0]))
                staged = [rows_to_vmem(source, 0, step)]
            gate, up = xor_reduce_scatter(first, "gy", ngy, 1, gy_levels[1:])
            if c == 0:
                for k in range(1, chunks):
                    source, _ = lax.optimization_barrier((w_down, gate))
                    staged.append(rows_to_vmem(source, k * step, step))
        else:
            gate = lax.psum_scatter(gate_part, "gy", scatter_dimension=1, tiled=True)
            up = lax.psum_scatter(up_part, "gy", scatter_dimension=1, tiled=True)
        hidden = (jax.nn.silu(gate) * up).astype(jnp.bfloat16)
        if pairwise(ngy):
            hidden_all = xor_all_gather(hidden, "gy", ngy, 1, gy_levels[::-1])
        else:
            hidden_all = lax.all_gather(hidden, "gy", axis=1, tiled=True)
        down = staged[c] if pairwise(ngy) else w_down[cols, :]
        term = jnp.dot(hidden_all, down, preferred_element_type=jnp.float32)
        total = term if total is None else total + term
    if pairwise(ngx):
        result = relative_reduce_scatter(total, "gx", ngx)
    else:
        result = lax.psum_scatter(total, "gx", scatter_dimension=0, tiled=True)
    return result.astype(jnp.bfloat16)


def solution(mesh):
    in_specs = (P(("groups", "gx"), "gy"), P("gy"), P("gy", "gx"), P("gy", "gx"), P("gx", "gy"))
    out_specs = P(("groups", "gx"), "gy")
    return jax.shard_map(local, mesh=mesh, in_specs=in_specs, out_specs=out_specs, check_vma=False)
```

```python
import jax
import jax.numpy as jnp
from jax import lax
from jax.experimental import pallas as pl
from jax.experimental.pallas import tpu as pltpu
from jax.sharding import PartitionSpec as P


epsilon = 1e-06

EXCHANGE_MAX = 8
CHUNKS = 2


def pairwise(n):
    return n <= EXCHANGE_MAX and n & (n - 1) == 0


def exchange(x, axis, n, s):
    return lax.ppermute(x, axis, [(a, a ^ (1 << s)) for a in range(n)])


def xor_reduce_scatter(parts, axis, n, dim, bits):
    me = lax.axis_index(axis)
    for s in bits:
        bit = (me >> s) & 1
        half = parts[0].shape[dim] // 2
        keep = [lax.dynamic_slice_in_dim(p, bit * half, half, axis=dim) for p in parts]
        send = [lax.dynamic_slice_in_dim(p, (1 - bit) * half, half, axis=dim) for p in parts]
        got = exchange(jnp.stack(send), axis, n, s)
        parts = [k + got[i] for i, k in enumerate(keep)]
    return parts


def xor_all_gather(x, axis, n, dim, bits):
    me = lax.axis_index(axis)
    for s in bits:
        other = exchange(x, axis, n, s)
        low = jnp.concatenate([x, other], axis=dim)
        high = jnp.concatenate([other, x], axis=dim)
        x = jnp.where(((me >> s) & 1) == 0, low, high)
    return x


def xor_all_reduce(x, axis, n):
    for s in range(n.bit_length() - 1):
        x = x + exchange(x, axis, n, s)
    return x


def gathered_position(d, bits):
    return sum(((d >> s) & 1) << t for t, s in enumerate(bits))


def fanout_reduce_scatter(x, axis, n, bits):
    me = lax.axis_index(axis)
    rows = x.shape[0] // n
    own = lax.dynamic_slice_in_dim(x, gathered_position(me, bits) * rows, rows, axis=0)
    for k in range(1, n):
        block = lax.dynamic_slice_in_dim(x, gathered_position(me ^ k, bits) * rows, rows, axis=0)
        own = own + lax.ppermute(block, axis, [(a, a ^ k) for a in range(n)])
    return own


def fanout_all_gather(x, axis, n, bits):
    me = lax.axis_index(axis)
    rows = x.shape[0]
    out = jnp.zeros((n * rows,) + x.shape[1:], x.dtype)
    for k in range(n):
        block = x if k == 0 else lax.ppermute(x, axis, [(a, a ^ k) for a in range(n)])
        out = lax.dynamic_update_slice_in_dim(out, block, gathered_position(me ^ k, bits) * rows, axis=0)
    return out


def fanout_all_reduce(x, axis, n):
    me = lax.axis_index(axis)
    got = jnp.stack([x] + [lax.ppermute(x, axis, [(a, a ^ k) for a in range(n)]) for k in range(1, n)])
    ordered = jnp.take(got, jnp.arange(n) ^ me, axis=0)
    return jnp.sum(ordered, axis=0)


def rows_to_vmem(w, start, count):
    size = count * w.shape[1] * w.dtype.itemsize

    def kernel(src, dst, sem):
        copy = pltpu.make_async_copy(src.at[pl.ds(start, count), :], dst, sem)
        copy.start()
        copy.wait()

    return pl.pallas_call(
        kernel,
        out_shape=jax.ShapeDtypeStruct((count, w.shape[1]), w.dtype),
        in_specs=[pl.BlockSpec(memory_space=pl.ANY)],
        out_specs=pl.BlockSpec(memory_space=pltpu.VMEM),
        scratch_shapes=[pltpu.SemaphoreType.DMA(())],
        cost_estimate=pl.CostEstimate(flops=0, transcendentals=0, bytes_accessed=2 * size),
        compiler_params=pltpu.CompilerParams(vmem_limit_bytes=size + (2 << 20)),
    )(pltpu.with_memory_space_constraint(w, pltpu.HBM))


def local(tokens, norm_gain, w_gate, w_up, w_down):
    ngx = lax.axis_size("gx")
    ngy = lax.axis_size("gy")
    features = tokens.shape[1] * ngy
    gx_levels = list(range(ngx.bit_length() - 1))
    values = tokens.astype(jnp.float32)
    local_sq = jnp.sum(values * values, axis=1)
    if pairwise(ngy):
        total_sq = fanout_all_reduce(local_sq, "gy", ngy)
    else:
        total_sq = lax.psum(local_sq, "gy")
    inverse = lax.rsqrt(total_sq / features + epsilon)
    normed = (values * inverse[:, None] * norm_gain[None, :]).astype(jnp.bfloat16)
    if pairwise(ngx):
        piece = fanout_all_gather(normed, "gx", ngx, gx_levels[::-1])
    else:
        piece = lax.all_gather(normed, "gx", axis=0, tiled=True)
    rows = piece.shape[0]

    width = w_gate.shape[1]
    chunks = CHUNKS if width % (CHUNKS * ngy * 128) == 0 else 1
    step = width // chunks
    gy_levels = list(range(ngy.bit_length() - 1))
    total = None
    for c in range(chunks):
        cols = slice(c * step, (c + 1) * step)
        gate_part = jnp.dot(piece, w_gate[:, cols], preferred_element_type=jnp.float32)
        up_part = jnp.dot(piece, w_up[:, cols], preferred_element_type=jnp.float32)
        if pairwise(ngy):
            first = xor_reduce_scatter([gate_part, up_part], "gy", ngy, 1, gy_levels[:1])
            if c == 0:
                source, _ = lax.optimization_barrier((w_down, first[0]))
                staged = [rows_to_vmem(source, 0, step)]
            gate, up = xor_reduce_scatter(first, "gy", ngy, 1, gy_levels[1:])
            if c == 0:
                for k in range(1, chunks):
                    source, _ = lax.optimization_barrier((w_down, gate))
                    staged.append(rows_to_vmem(source, k * step, step))
        else:
            gate = lax.psum_scatter(gate_part, "gy", scatter_dimension=1, tiled=True)
            up = lax.psum_scatter(up_part, "gy", scatter_dimension=1, tiled=True)
        hidden = (jax.nn.silu(gate) * up).astype(jnp.bfloat16)
        if pairwise(ngy):
            hidden_all = xor_all_gather(hidden, "gy", ngy, 1, gy_levels[::-1])
        else:
            hidden_all = lax.all_gather(hidden, "gy", axis=1, tiled=True)
        down = staged[c] if pairwise(ngy) else w_down[cols, :]
        term = jnp.dot(hidden_all, down, preferred_element_type=jnp.float32)
        total = term if total is None else total + term
    if pairwise(ngx):
        result = fanout_reduce_scatter(total, "gx", ngx, gx_levels[::-1])
    else:
        result = lax.psum_scatter(total, "gx", scatter_dimension=0, tiled=True)
    return result.astype(jnp.bfloat16)


def solution(mesh):
    in_specs = (P(("groups", "gx"), "gy"), P("gy"), P("gy", "gx"), P("gy", "gx"), P("gx", "gy"))
    out_specs = P(("groups", "gx"), "gy")
    return jax.shard_map(local, mesh=mesh, in_specs=in_specs, out_specs=out_specs, check_vma=False)
```

```python
import jax
import jax.numpy as jnp
from jax import lax
from jax.experimental import pallas as pl
from jax.experimental.pallas import tpu as pltpu
from jax.sharding import PartitionSpec as P


epsilon = 1e-06

EXCHANGE_MAX = 8
CHUNKS = 2


def pairwise(n):
    return n <= EXCHANGE_MAX and n & (n - 1) == 0


def exchange(x, axis, n, s):
    return lax.ppermute(x, axis, [(a, a ^ (1 << s)) for a in range(n)])


def xor_reduce_scatter(parts, axis, n, dim, bits):
    me = lax.axis_index(axis)
    for s in bits:
        bit = (me >> s) & 1
        half = parts[0].shape[dim] // 2
        keep = [lax.dynamic_slice_in_dim(p, bit * half, half, axis=dim) for p in parts]
        send = [lax.dynamic_slice_in_dim(p, (1 - bit) * half, half, axis=dim) for p in parts]
        got = exchange(jnp.stack(send), axis, n, s)
        parts = [k + got[i] for i, k in enumerate(keep)]
    return parts


def xor_all_gather(x, axis, n, dim, bits):
    me = lax.axis_index(axis)
    for s in bits:
        other = exchange(x, axis, n, s)
        low = jnp.concatenate([x, other], axis=dim)
        high = jnp.concatenate([other, x], axis=dim)
        x = jnp.where(((me >> s) & 1) == 0, low, high)
    return x


def xor_all_reduce(x, axis, n):
    for s in range(n.bit_length() - 1):
        x = x + exchange(x, axis, n, s)
    return x


def gathered_position(d, bits):
    return sum(((d >> s) & 1) << t for t, s in enumerate(bits))


def fanout_reduce_scatter(x, axis, n, bits):
    me = lax.axis_index(axis)
    rows = x.shape[0] // n
    own = lax.dynamic_slice_in_dim(x, gathered_position(me, bits) * rows, rows, axis=0)
    for k in range(1, n):
        block = lax.dynamic_slice_in_dim(x, gathered_position(me ^ k, bits) * rows, rows, axis=0)
        own = own + lax.ppermute(block, axis, [(a, a ^ k) for a in range(n)])
    return own


def fanout_all_gather(x, axis, n, bits):
    me = lax.axis_index(axis)
    rows = x.shape[0]
    out = jnp.zeros((n * rows,) + x.shape[1:], x.dtype)
    for k in range(n):
        block = x if k == 0 else lax.ppermute(x, axis, [(a, a ^ k) for a in range(n)])
        out = lax.dynamic_update_slice_in_dim(out, block, gathered_position(me ^ k, bits) * rows, axis=0)
    return out


def fanout_all_reduce(x, axis, n):
    me = lax.axis_index(axis)
    got = jnp.stack([x] + [lax.ppermute(x, axis, [(a, a ^ k) for a in range(n)]) for k in range(1, n)])
    ordered = jnp.take(got, jnp.arange(n) ^ me, axis=0)
    return jnp.sum(ordered, axis=0)


def rows_to_vmem(w, start, count):
    size = count * w.shape[1] * w.dtype.itemsize

    def kernel(src, dst, sem):
        copy = pltpu.make_async_copy(src.at[pl.ds(start, count), :], dst, sem)
        copy.start()
        copy.wait()

    return pl.pallas_call(
        kernel,
        out_shape=jax.ShapeDtypeStruct((count, w.shape[1]), w.dtype),
        in_specs=[pl.BlockSpec(memory_space=pl.ANY)],
        out_specs=pl.BlockSpec(memory_space=pltpu.VMEM),
        scratch_shapes=[pltpu.SemaphoreType.DMA(())],
        cost_estimate=pl.CostEstimate(flops=0, transcendentals=0, bytes_accessed=2 * size),
        compiler_params=pltpu.CompilerParams(vmem_limit_bytes=size + (2 << 20)),
    )(pltpu.with_memory_space_constraint(w, pltpu.HBM))


def local(tokens, norm_gain, w_gate, w_up, w_down):
    ngx = lax.axis_size("gx")
    ngy = lax.axis_size("gy")
    features = tokens.shape[1] * ngy
    gx_levels = list(range(ngx.bit_length() - 1))
    if pairwise(ngx):
        raw = fanout_all_gather(tokens, "gx", ngx, gx_levels[::-1])
    else:
        raw = lax.all_gather(tokens, "gx", axis=0, tiled=True)
    values = raw.astype(jnp.float32)
    local_sq = jnp.sum(values * values, axis=1)
    if pairwise(ngy):
        total_sq = fanout_all_reduce(local_sq, "gy", ngy)
    else:
        total_sq = lax.psum(local_sq, "gy")
    inverse = lax.rsqrt(total_sq / features + epsilon)
    piece = (values * inverse[:, None] * norm_gain[None, :]).astype(jnp.bfloat16)
    rows = piece.shape[0]

    width = w_gate.shape[1]
    chunks = CHUNKS if width % (CHUNKS * ngy * 128) == 0 else 1
    step = width // chunks
    gy_levels = list(range(ngy.bit_length() - 1))
    total = None
    pieces = {}
    staged = None
    downs = []
    for c in range(chunks):
        cols = slice(c * step, (c + 1) * step)
        gate_part = jnp.dot(piece, w_gate[:, cols], preferred_element_type=jnp.float32)
        up_part = jnp.dot(piece, w_up[:, cols], preferred_element_type=jnp.float32)
        if pairwise(ngy):
            first = xor_reduce_scatter([gate_part, up_part], "gy", ngy, 1, gy_levels[:1])
            quarter = step // 2
            source, _ = lax.optimization_barrier((w_down, first[0]))
            pieces[c] = [rows_to_vmem(source, c * quarter, quarter)]
            gate, up = xor_reduce_scatter(first, "gy", ngy, 1, gy_levels[1:])
            source, _ = lax.optimization_barrier((w_down, gate))
            pieces[c].append(rows_to_vmem(source, (chunks + c) * quarter, quarter))
            if c == chunks - 1:
                flat = [pieces[k][0] for k in range(chunks)] + [pieces[k][1] for k in range(chunks)]
                staged = [flat[2 * k:2 * k + 2] for k in range(chunks)]
        else:
            gate = lax.psum_scatter(gate_part, "gy", scatter_dimension=1, tiled=True)
            up = lax.psum_scatter(up_part, "gy", scatter_dimension=1, tiled=True)
        hidden = (jax.nn.silu(gate) * up).astype(jnp.bfloat16)
        if pairwise(ngy):
            hidden_all = xor_all_gather(hidden, "gy", ngy, 1, gy_levels[::-1])
        else:
            hidden_all = lax.all_gather(hidden, "gy", axis=1, tiled=True)
        downs.append(hidden_all)
    for c in range(chunks):
        hidden_all = downs[c]
        if pairwise(ngy):
            half = step // 2
            term = (jnp.dot(hidden_all[:, :half], staged[c][0], preferred_element_type=jnp.float32)
                    + jnp.dot(hidden_all[:, half:], staged[c][1], preferred_element_type=jnp.float32))
        else:
            term = jnp.dot(hidden_all, w_down[c * step:(c + 1) * step, :], preferred_element_type=jnp.float32)
        total = term if total is None else total + term
    if pairwise(ngx):
        result = fanout_reduce_scatter(total, "gx", ngx, gx_levels[::-1])
    else:
        result = lax.psum_scatter(total, "gx", scatter_dimension=0, tiled=True)
    return result.astype(jnp.bfloat16)


def solution(mesh):
    in_specs = (P(("groups", "gx"), "gy"), P("gy"), P("gy", "gx"), P("gy", "gx"), P("gx", "gy"))
    out_specs = P(("groups", "gx"), "gy")
    return jax.shard_map(local, mesh=mesh, in_specs=in_specs, out_specs=out_specs, check_vma=False)
```

```python
import jax
import jax.numpy as jnp
from jax import lax
from jax.experimental import pallas as pl
from jax.experimental.pallas import tpu as pltpu
from jax.sharding import PartitionSpec as P


epsilon = 1e-06

EXCHANGE_MAX = 8
CHUNKS = 2


def pairwise(n):
    return n <= EXCHANGE_MAX and n & (n - 1) == 0


def exchange(x, axis, n, s):
    return lax.ppermute(x, axis, [(a, a ^ (1 << s)) for a in range(n)])


def xor_reduce_scatter(parts, axis, n, dim, bits):
    me = lax.axis_index(axis)
    for s in bits:
        bit = (me >> s) & 1
        half = parts[0].shape[dim] // 2
        keep = [lax.dynamic_slice_in_dim(p, bit * half, half, axis=dim) for p in parts]
        send = [lax.dynamic_slice_in_dim(p, (1 - bit) * half, half, axis=dim) for p in parts]
        got = exchange(jnp.stack(send), axis, n, s)
        parts = [k + got[i] for i, k in enumerate(keep)]
    return parts


def xor_all_gather(x, axis, n, dim, bits):
    me = lax.axis_index(axis)
    for s in bits:
        other = exchange(x, axis, n, s)
        low = jnp.concatenate([x, other], axis=dim)
        high = jnp.concatenate([other, x], axis=dim)
        x = jnp.where(((me >> s) & 1) == 0, low, high)
    return x


def xor_all_reduce(x, axis, n):
    for s in range(n.bit_length() - 1):
        x = x + exchange(x, axis, n, s)
    return x


def gathered_position(d, bits):
    return sum(((d >> s) & 1) << t for t, s in enumerate(bits))


def fanout_reduce_scatter(x, axis, n, bits):
    me = lax.axis_index(axis)
    rows = x.shape[0] // n
    own = lax.dynamic_slice_in_dim(x, gathered_position(me, bits) * rows, rows, axis=0)
    for k in range(1, n):
        block = lax.dynamic_slice_in_dim(x, gathered_position(me ^ k, bits) * rows, rows, axis=0)
        own = own + lax.ppermute(block, axis, [(a, a ^ k) for a in range(n)])
    return own


def fanout_all_gather(x, axis, n, bits):
    me = lax.axis_index(axis)
    blocks = jnp.stack([x] + [lax.ppermute(x, axis, [(a, a ^ k) for a in range(n)]) for k in range(1, n)])
    owner = [next(d for d in range(n) if gathered_position(d, bits) == p) for p in range(n)]
    ordered = jnp.take(blocks, jnp.asarray(owner, jnp.int32) ^ me, axis=0)
    return ordered.reshape((n * x.shape[0],) + x.shape[1:])


def fanout_all_reduce(x, axis, n):
    me = lax.axis_index(axis)
    got = jnp.stack([x] + [lax.ppermute(x, axis, [(a, a ^ k) for a in range(n)]) for k in range(1, n)])
    ordered = jnp.take(got, jnp.arange(n) ^ me, axis=0)
    return jnp.sum(ordered, axis=0)


def rows_to_vmem(w, start, count):
    size = count * w.shape[1] * w.dtype.itemsize

    def kernel(src, dst, sem):
        copy = pltpu.make_async_copy(src.at[pl.ds(start, count), :], dst, sem)
        copy.start()
        copy.wait()

    return pl.pallas_call(
        kernel,
        out_shape=jax.ShapeDtypeStruct((count, w.shape[1]), w.dtype),
        in_specs=[pl.BlockSpec(memory_space=pl.ANY)],
        out_specs=pl.BlockSpec(memory_space=pltpu.VMEM),
        scratch_shapes=[pltpu.SemaphoreType.DMA(())],
        cost_estimate=pl.CostEstimate(flops=0, transcendentals=0, bytes_accessed=2 * size),
        compiler_params=pltpu.CompilerParams(vmem_limit_bytes=size + (2 << 20)),
    )(pltpu.with_memory_space_constraint(w, pltpu.HBM))


def local(tokens, norm_gain, w_gate, w_up, w_down):
    ngx = lax.axis_size("gx")
    ngy = lax.axis_size("gy")
    features = tokens.shape[1] * ngy
    gx_levels = list(range(ngx.bit_length() - 1))
    if pairwise(ngx):
        raw = fanout_all_gather(tokens, "gx", ngx, gx_levels[::-1])
    else:
        raw = lax.all_gather(tokens, "gx", axis=0, tiled=True)
    values = raw.astype(jnp.float32)
    local_sq = jnp.sum(values * values, axis=1)
    if pairwise(ngy):
        total_sq = fanout_all_reduce(local_sq, "gy", ngy)
    else:
        total_sq = lax.psum(local_sq, "gy")
    inverse = lax.rsqrt(total_sq / features + epsilon)
    piece = (values * inverse[:, None] * norm_gain[None, :]).astype(jnp.bfloat16)
    rows = piece.shape[0]

    width = w_gate.shape[1]
    chunks = CHUNKS if width % (CHUNKS * ngy * 128) == 0 else 1
    step = width // chunks
    gy_levels = list(range(ngy.bit_length() - 1))
    total = None
    for c in range(chunks):
        cols = slice(c * step, (c + 1) * step)
        gate_part = jnp.dot(piece, w_gate[:, cols], preferred_element_type=jnp.float32)
        up_part = jnp.dot(piece, w_up[:, cols], preferred_element_type=jnp.float32)
        if pairwise(ngy):
            first = xor_reduce_scatter([gate_part, up_part], "gy", ngy, 1, gy_levels[:1])
            if c == 0:
                source, _ = lax.optimization_barrier((w_down, first[0]))
                staged = [rows_to_vmem(source, 0, step)]
            gate, up = xor_reduce_scatter(first, "gy", ngy, 1, gy_levels[1:])
            if c == 0:
                for k in range(1, chunks):
                    source, _ = lax.optimization_barrier((w_down, gate))
                    staged.append(rows_to_vmem(source, k * step, step))
        else:
            gate = lax.psum_scatter(gate_part, "gy", scatter_dimension=1, tiled=True)
            up = lax.psum_scatter(up_part, "gy", scatter_dimension=1, tiled=True)
        hidden = (jax.nn.silu(gate) * up).astype(jnp.bfloat16)
        if pairwise(ngy):
            hidden_all = xor_all_gather(hidden, "gy", ngy, 1, gy_levels[::-1])
        else:
            hidden_all = lax.all_gather(hidden, "gy", axis=1, tiled=True)
        down = staged[c] if pairwise(ngy) else w_down[cols, :]
        term = jnp.dot(hidden_all, down, preferred_element_type=jnp.float32)
        total = term if total is None else total + term
    if pairwise(ngx):
        result = fanout_reduce_scatter(total, "gx", ngx, gx_levels[::-1])
    else:
        result = lax.psum_scatter(total, "gx", scatter_dimension=0, tiled=True)
    return result.astype(jnp.bfloat16)


def solution(mesh):
    in_specs = (P(("groups", "gx"), "gy"), P("gy"), P("gy", "gx"), P("gy", "gx"), P("gx", "gy"))
    out_specs = P(("groups", "gx"), "gy")
    return jax.shard_map(local, mesh=mesh, in_specs=in_specs, out_specs=out_specs, check_vma=False)
```

```python
import jax
import jax.numpy as jnp
from jax import lax
from jax.experimental import pallas as pl
from jax.experimental.pallas import tpu as pltpu
from jax.sharding import PartitionSpec as P


epsilon = 1e-06

EXCHANGE_MAX = 8
CHUNKS = 2


def pairwise(n):
    return n <= EXCHANGE_MAX and n & (n - 1) == 0


def exchange(x, axis, n, s):
    return lax.ppermute(x, axis, [(a, a ^ (1 << s)) for a in range(n)])


def xor_reduce_scatter(parts, axis, n, dim, bits):
    me = lax.axis_index(axis)
    for s in bits:
        bit = (me >> s) & 1
        half = parts[0].shape[dim] // 2
        keep = [lax.dynamic_slice_in_dim(p, bit * half, half, axis=dim) for p in parts]
        send = [lax.dynamic_slice_in_dim(p, (1 - bit) * half, half, axis=dim) for p in parts]
        got = exchange(jnp.stack(send), axis, n, s)
        parts = [k + got[i] for i, k in enumerate(keep)]
    return parts


def xor_all_gather(x, axis, n, dim, bits):
    me = lax.axis_index(axis)
    for s in bits:
        other = exchange(x, axis, n, s)
        low = jnp.concatenate([x, other], axis=dim)
        high = jnp.concatenate([other, x], axis=dim)
        x = jnp.where(((me >> s) & 1) == 0, low, high)
    return x


def xor_all_reduce(x, axis, n):
    for s in range(n.bit_length() - 1):
        x = x + exchange(x, axis, n, s)
    return x


def gathered_position(d, bits):
    return sum(((d >> s) & 1) << t for t, s in enumerate(bits))


def fanout_reduce_scatter(x, axis, n, bits):
    me = lax.axis_index(axis)
    rows = x.shape[0] // n
    own = lax.dynamic_slice_in_dim(x, gathered_position(me, bits) * rows, rows, axis=0)
    for k in range(1, n):
        block = lax.dynamic_slice_in_dim(x, gathered_position(me ^ k, bits) * rows, rows, axis=0)
        own = own + lax.ppermute(block, axis, [(a, a ^ k) for a in range(n)])
    return own


def fanout_all_gather(x, axis, n, bits):
    me = lax.axis_index(axis)
    rows = x.shape[0]
    out = jnp.zeros((n * rows,) + x.shape[1:], x.dtype)
    for k in range(n):
        block = x if k == 0 else lax.ppermute(x, axis, [(a, a ^ k) for a in range(n)])
        out = lax.dynamic_update_slice_in_dim(out, block, gathered_position(me ^ k, bits) * rows, axis=0)
    return out


def fanout_all_reduce(x, axis, n):
    me = lax.axis_index(axis)
    got = jnp.stack([x] + [lax.ppermute(x, axis, [(a, a ^ k) for a in range(n)]) for k in range(1, n)])
    ordered = jnp.take(got, jnp.arange(n) ^ me, axis=0)
    return jnp.sum(ordered, axis=0)


def rows_to_vmem(w, start, count):
    size = count * w.shape[1] * w.dtype.itemsize

    def kernel(src, dst, sem):
        copy = pltpu.make_async_copy(src.at[pl.ds(start, count), :], dst, sem)
        copy.start()
        copy.wait()

    return pl.pallas_call(
        kernel,
        out_shape=jax.ShapeDtypeStruct((count, w.shape[1]), w.dtype),
        in_specs=[pl.BlockSpec(memory_space=pl.ANY)],
        out_specs=pl.BlockSpec(memory_space=pltpu.VMEM),
        scratch_shapes=[pltpu.SemaphoreType.DMA(())],
        cost_estimate=pl.CostEstimate(flops=0, transcendentals=0, bytes_accessed=2 * size),
        compiler_params=pltpu.CompilerParams(vmem_limit_bytes=size + (2 << 20)),
    )(pltpu.with_memory_space_constraint(w, pltpu.HBM))


def local(tokens, norm_gain, w_gate, w_up, w_down):
    ngx = lax.axis_size("gx")
    ngy = lax.axis_size("gy")
    features = tokens.shape[1] * ngy
    gx_levels = list(range(ngx.bit_length() - 1))
    if pairwise(ngx):
        raw = fanout_all_gather(tokens, "gx", ngx, gx_levels[::-1])
    else:
        raw = lax.all_gather(tokens, "gx", axis=0, tiled=True)
    values = raw.astype(jnp.float32)
    local_sq = jnp.sum(values * values, axis=1)
    if pairwise(ngy):
        total_sq = fanout_all_reduce(local_sq, "gy", ngy)
    else:
        total_sq = lax.psum(local_sq, "gy")
    inverse = lax.rsqrt(total_sq / features + epsilon)
    piece = (values * inverse[:, None] * norm_gain[None, :]).astype(jnp.bfloat16)
    rows = piece.shape[0]

    width = w_gate.shape[1]
    chunks = CHUNKS if width % (CHUNKS * ngy * 128) == 0 else 1
    step = width // chunks
    gy_levels = list(range(ngy.bit_length() - 1))
    total = None
    for c in range(chunks):
        cols = slice(c * step, (c + 1) * step)
        gate_part = jnp.dot(piece, w_gate[:, cols], preferred_element_type=jnp.float32)
        up_part = jnp.dot(piece, w_up[:, cols], preferred_element_type=jnp.float32)
        if pairwise(ngy):
            first = xor_reduce_scatter([gate_part, up_part], "gy", ngy, 1, gy_levels[:1])
            if c == 0:
                source, _ = lax.optimization_barrier((w_down, first[0]))
                staged = [rows_to_vmem(source, 0, step)]
            gate, up = xor_reduce_scatter(first, "gy", ngy, 1, gy_levels[1:])
            if c == chunks - 1:
                for k in range(1, chunks):
                    source, _ = lax.optimization_barrier((w_down, gate))
                    staged.append(rows_to_vmem(source, k * step, step))
        else:
            gate = lax.psum_scatter(gate_part, "gy", scatter_dimension=1, tiled=True)
            up = lax.psum_scatter(up_part, "gy", scatter_dimension=1, tiled=True)
        hidden = (jax.nn.silu(gate) * up).astype(jnp.bfloat16)
        if pairwise(ngy):
            hidden_all = xor_all_gather(hidden, "gy", ngy, 1, gy_levels[::-1])
        else:
            hidden_all = lax.all_gather(hidden, "gy", axis=1, tiled=True)
        down = staged[c] if pairwise(ngy) else w_down[cols, :]
        term = jnp.dot(hidden_all, down, preferred_element_type=jnp.float32)
        total = term if total is None else total + term
    if pairwise(ngx):
        result = fanout_reduce_scatter(total, "gx", ngx, gx_levels[::-1])
    else:
        result = lax.psum_scatter(total, "gx", scatter_dimension=0, tiled=True)
    return result.astype(jnp.bfloat16)


def solution(mesh):
    in_specs = (P(("groups", "gx"), "gy"), P("gy"), P("gy", "gx"), P("gy", "gx"), P("gx", "gy"))
    out_specs = P(("groups", "gx"), "gy")
    return jax.shard_map(local, mesh=mesh, in_specs=in_specs, out_specs=out_specs, check_vma=False)
```

```python
import jax
import jax.numpy as jnp
from jax import lax
from jax.experimental import pallas as pl
from jax.experimental.pallas import tpu as pltpu
from jax.sharding import PartitionSpec as P


epsilon = 1e-06

EXCHANGE_MAX = 8
CHUNKS = 2


def pairwise(n):
    return n <= EXCHANGE_MAX and n & (n - 1) == 0


def exchange(x, axis, n, s):
    return lax.ppermute(x, axis, [(a, a ^ (1 << s)) for a in range(n)])


def xor_reduce_scatter(parts, axis, n, dim, bits):
    me = lax.axis_index(axis)
    for s in bits:
        bit = (me >> s) & 1
        half = parts[0].shape[dim] // 2
        keep = [lax.dynamic_slice_in_dim(p, bit * half, half, axis=dim) for p in parts]
        send = [lax.dynamic_slice_in_dim(p, (1 - bit) * half, half, axis=dim) for p in parts]
        got = exchange(jnp.stack(send), axis, n, s)
        parts = [k + got[i] for i, k in enumerate(keep)]
    return parts


def xor_all_gather(x, axis, n, dim, bits):
    me = lax.axis_index(axis)
    for s in bits:
        other = exchange(x, axis, n, s)
        low = jnp.concatenate([x, other], axis=dim)
        high = jnp.concatenate([other, x], axis=dim)
        x = jnp.where(((me >> s) & 1) == 0, low, high)
    return x


def xor_all_reduce(x, axis, n):
    for s in range(n.bit_length() - 1):
        x = x + exchange(x, axis, n, s)
    return x


def gathered_position(d, bits):
    return sum(((d >> s) & 1) << t for t, s in enumerate(bits))


def fanout_reduce_scatter(x, axis, n, bits):
    me = lax.axis_index(axis)
    rows = x.shape[0] // n
    own = lax.dynamic_slice_in_dim(x, gathered_position(me, bits) * rows, rows, axis=0)
    for k in range(1, n):
        block = lax.dynamic_slice_in_dim(x, gathered_position(me ^ k, bits) * rows, rows, axis=0)
        own = own + lax.ppermute(block, axis, [(a, a ^ k) for a in range(n)])
    return own


def fanout_all_gather(x, axis, n, bits):
    me = lax.axis_index(axis)
    rows = x.shape[0]
    out = jnp.zeros((n * rows,) + x.shape[1:], x.dtype)
    for k in range(n):
        block = x if k == 0 else lax.ppermute(x, axis, [(a, a ^ k) for a in range(n)])
        out = lax.dynamic_update_slice_in_dim(out, block, gathered_position(me ^ k, bits) * rows, axis=0)
    return out


def fanout_all_reduce(x, axis, n):
    me = lax.axis_index(axis)
    got = jnp.stack([x] + [lax.ppermute(x, axis, [(a, a ^ k) for a in range(n)]) for k in range(1, n)])
    ordered = jnp.take(got, jnp.arange(n) ^ me, axis=0)
    return jnp.sum(ordered, axis=0)


def rows_to_vmem(w, start, count):
    size = count * w.shape[1] * w.dtype.itemsize

    def kernel(src, dst, sem):
        copy = pltpu.make_async_copy(src.at[pl.ds(start, count), :], dst, sem)
        copy.start()
        copy.wait()

    return pl.pallas_call(
        kernel,
        out_shape=jax.ShapeDtypeStruct((count, w.shape[1]), w.dtype),
        in_specs=[pl.BlockSpec(memory_space=pl.ANY)],
        out_specs=pl.BlockSpec(memory_space=pltpu.VMEM),
        scratch_shapes=[pltpu.SemaphoreType.DMA(())],
        cost_estimate=pl.CostEstimate(flops=0, transcendentals=0, bytes_accessed=2 * size),
        compiler_params=pltpu.CompilerParams(vmem_limit_bytes=size + (2 << 20)),
    )(pltpu.with_memory_space_constraint(w, pltpu.HBM))


def local(tokens, norm_gain, w_gate, w_up, w_down):
    ngx = lax.axis_size("gx")
    ngy = lax.axis_size("gy")
    features = tokens.shape[1] * ngy
    gx_levels = list(range(ngx.bit_length() - 1))
    if pairwise(ngx):
        raw = fanout_all_gather(tokens, "gx", ngx, gx_levels[::-1])
    else:
        raw = lax.all_gather(tokens, "gx", axis=0, tiled=True)
    values = raw.astype(jnp.float32)
    local_sq = jnp.sum(values * values, axis=1)
    if pairwise(ngy):
        total_sq = fanout_all_reduce(local_sq, "gy", ngy)
    else:
        total_sq = lax.psum(local_sq, "gy")
    inverse = lax.rsqrt(total_sq / features + epsilon)
    piece = (values * inverse[:, None] * norm_gain[None, :]).astype(jnp.bfloat16)
    rows = piece.shape[0]

    width = w_gate.shape[1]
    chunks = CHUNKS if width % (CHUNKS * ngy * 128) == 0 else 1
    step = width // chunks
    gy_levels = list(range(ngy.bit_length() - 1))
    total = None
    if pairwise(ngy) and ngy >= 4:
        me = lax.axis_index("gy")
        parts = []
        for c in range(chunks):
            cols = slice(c * step, (c + 1) * step)
            parts.append(jnp.dot(piece, w_gate[:, cols], preferred_element_type=jnp.float32))
            parts.append(jnp.dot(piece, w_up[:, cols], preferred_element_type=jnp.float32))
        first = xor_reduce_scatter(parts, "gy", ngy, 1, gy_levels[:1])
        source, _ = lax.optimization_barrier((w_down, first[0]))
        staged = [rows_to_vmem(source, 0, step)]
        sums = []
        for c in range(chunks):
            sums.append(xor_reduce_scatter(first[2 * c:2 * c + 2], "gy", ngy, 1, gy_levels[1:]))
            if c == 0:
                for k in range(1, chunks):
                    source, _ = lax.optimization_barrier((w_down, sums[0][0]))
                    staged.append(rows_to_vmem(source, k * step, step))
        halves = []
        for gate, up in sums:
            hidden = (jax.nn.silu(gate) * up).astype(jnp.bfloat16)
            halves.append(xor_all_gather(hidden, "gy", ngy, 1, gy_levels[1:][::-1]))
        others = exchange(jnp.stack(halves), "gy", ngy, gy_levels[0])
        low = (me & 1) == 0
        for c in range(chunks):
            mine, other = halves[c], others[c]
            hidden_all = jnp.where(low, jnp.concatenate([mine, other], axis=1),
                                   jnp.concatenate([other, mine], axis=1))
            term = jnp.dot(hidden_all, staged[c], preferred_element_type=jnp.float32)
            total = term if total is None else total + term
    else:
        for c in range(chunks):
            cols = slice(c * step, (c + 1) * step)
            gate_part = jnp.dot(piece, w_gate[:, cols], preferred_element_type=jnp.float32)
            up_part = jnp.dot(piece, w_up[:, cols], preferred_element_type=jnp.float32)
            if pairwise(ngy):
                gate, up = xor_reduce_scatter([gate_part, up_part], "gy", ngy, 1, gy_levels)
            else:
                gate = lax.psum_scatter(gate_part, "gy", scatter_dimension=1, tiled=True)
                up = lax.psum_scatter(up_part, "gy", scatter_dimension=1, tiled=True)
            hidden = (jax.nn.silu(gate) * up).astype(jnp.bfloat16)
            if pairwise(ngy):
                hidden_all = xor_all_gather(hidden, "gy", ngy, 1, gy_levels[::-1])
            else:
                hidden_all = lax.all_gather(hidden, "gy", axis=1, tiled=True)
            term = jnp.dot(hidden_all, w_down[cols, :], preferred_element_type=jnp.float32)
            total = term if total is None else total + term
    if pairwise(ngx):
        result = fanout_reduce_scatter(total, "gx", ngx, gx_levels[::-1])
    else:
        result = lax.psum_scatter(total, "gx", scatter_dimension=0, tiled=True)
    return result.astype(jnp.bfloat16)


def solution(mesh):
    in_specs = (P(("groups", "gx"), "gy"), P("gy"), P("gy", "gx"), P("gy", "gx"), P("gx", "gy"))
    out_specs = P(("groups", "gx"), "gy")
    return jax.shard_map(local, mesh=mesh, in_specs=in_specs, out_specs=out_specs, check_vma=False)
```

```python
import jax
import jax.numpy as jnp
from jax import lax
from jax.experimental import pallas as pl
from jax.experimental.pallas import tpu as pltpu
from jax.sharding import PartitionSpec as P


epsilon = 1e-06

EXCHANGE_MAX = 8
CHUNKS = 3


def pairwise(n):
    return n <= EXCHANGE_MAX and n & (n - 1) == 0


def exchange(x, axis, n, s):
    return lax.ppermute(x, axis, [(a, a ^ (1 << s)) for a in range(n)])


def xor_reduce_scatter(parts, axis, n, dim, bits):
    me = lax.axis_index(axis)
    for s in bits:
        bit = (me >> s) & 1
        half = parts[0].shape[dim] // 2
        keep = [lax.dynamic_slice_in_dim(p, bit * half, half, axis=dim) for p in parts]
        send = [lax.dynamic_slice_in_dim(p, (1 - bit) * half, half, axis=dim) for p in parts]
        got = exchange(jnp.stack(send), axis, n, s)
        parts = [k + got[i] for i, k in enumerate(keep)]
    return parts


def xor_all_gather(x, axis, n, dim, bits):
    me = lax.axis_index(axis)
    for s in bits:
        other = exchange(x, axis, n, s)
        low = jnp.concatenate([x, other], axis=dim)
        high = jnp.concatenate([other, x], axis=dim)
        x = jnp.where(((me >> s) & 1) == 0, low, high)
    return x


def xor_all_reduce(x, axis, n):
    for s in range(n.bit_length() - 1):
        x = x + exchange(x, axis, n, s)
    return x


def gathered_position(d, bits):
    return sum(((d >> s) & 1) << t for t, s in enumerate(bits))


def fanout_reduce_scatter(x, axis, n, bits):
    me = lax.axis_index(axis)
    rows = x.shape[0] // n
    own = lax.dynamic_slice_in_dim(x, gathered_position(me, bits) * rows, rows, axis=0)
    for k in range(1, n):
        block = lax.dynamic_slice_in_dim(x, gathered_position(me ^ k, bits) * rows, rows, axis=0)
        own = own + lax.ppermute(block, axis, [(a, a ^ k) for a in range(n)])
    return own


def fanout_all_gather(x, axis, n, bits):
    me = lax.axis_index(axis)
    rows = x.shape[0]
    out = jnp.zeros((n * rows,) + x.shape[1:], x.dtype)
    for k in range(n):
        block = x if k == 0 else lax.ppermute(x, axis, [(a, a ^ k) for a in range(n)])
        out = lax.dynamic_update_slice_in_dim(out, block, gathered_position(me ^ k, bits) * rows, axis=0)
    return out


def fanout_all_reduce(x, axis, n):
    me = lax.axis_index(axis)
    got = jnp.stack([x] + [lax.ppermute(x, axis, [(a, a ^ k) for a in range(n)]) for k in range(1, n)])
    ordered = jnp.take(got, jnp.arange(n) ^ me, axis=0)
    return jnp.sum(ordered, axis=0)


def rows_to_vmem(w, start, count):
    size = count * w.shape[1] * w.dtype.itemsize

    def kernel(src, dst, sem):
        copy = pltpu.make_async_copy(src.at[pl.ds(start, count), :], dst, sem)
        copy.start()
        copy.wait()

    return pl.pallas_call(
        kernel,
        out_shape=jax.ShapeDtypeStruct((count, w.shape[1]), w.dtype),
        in_specs=[pl.BlockSpec(memory_space=pl.ANY)],
        out_specs=pl.BlockSpec(memory_space=pltpu.VMEM),
        scratch_shapes=[pltpu.SemaphoreType.DMA(())],
        cost_estimate=pl.CostEstimate(flops=0, transcendentals=0, bytes_accessed=2 * size),
        compiler_params=pltpu.CompilerParams(vmem_limit_bytes=size + (2 << 20)),
    )(pltpu.with_memory_space_constraint(w, pltpu.HBM))


def local(tokens, norm_gain, w_gate, w_up, w_down):
    ngx = lax.axis_size("gx")
    ngy = lax.axis_size("gy")
    features = tokens.shape[1] * ngy
    gx_levels = list(range(ngx.bit_length() - 1))
    if pairwise(ngx):
        raw = fanout_all_gather(tokens, "gx", ngx, gx_levels[::-1])
    else:
        raw = lax.all_gather(tokens, "gx", axis=0, tiled=True)
    values = raw.astype(jnp.float32)
    local_sq = jnp.sum(values * values, axis=1)
    if pairwise(ngy):
        total_sq = fanout_all_reduce(local_sq, "gy", ngy)
    else:
        total_sq = lax.psum(local_sq, "gy")
    inverse = lax.rsqrt(total_sq / features + epsilon)
    piece = (values * inverse[:, None] * norm_gain[None, :]).astype(jnp.bfloat16)
    rows = piece.shape[0]

    width = w_gate.shape[1]
    chunks = CHUNKS if width % (CHUNKS * ngy * 128) == 0 else 1
    step = width // chunks
    gy_levels = list(range(ngy.bit_length() - 1))
    total = None
    for c in range(chunks):
        cols = slice(c * step, (c + 1) * step)
        gate_part = jnp.dot(piece, w_gate[:, cols], preferred_element_type=jnp.float32)
        up_part = jnp.dot(piece, w_up[:, cols], preferred_element_type=jnp.float32)
        if pairwise(ngy):
            first = xor_reduce_scatter([gate_part, up_part], "gy", ngy, 1, gy_levels[:1])
            if c == 0:
                source, _ = lax.optimization_barrier((w_down, first[0]))
                staged = [rows_to_vmem(source, 0, step)]
            gate, up = xor_reduce_scatter(first, "gy", ngy, 1, gy_levels[1:])
            if c == 0:
                for k in range(1, chunks):
                    source, _ = lax.optimization_barrier((w_down, gate))
                    staged.append(rows_to_vmem(source, k * step, step))
        else:
            gate = lax.psum_scatter(gate_part, "gy", scatter_dimension=1, tiled=True)
            up = lax.psum_scatter(up_part, "gy", scatter_dimension=1, tiled=True)
        hidden = (jax.nn.silu(gate) * up).astype(jnp.bfloat16)
        if pairwise(ngy):
            hidden_all = xor_all_gather(hidden, "gy", ngy, 1, gy_levels[::-1])
        else:
            hidden_all = lax.all_gather(hidden, "gy", axis=1, tiled=True)
        down = staged[c] if pairwise(ngy) else w_down[cols, :]
        term = jnp.dot(hidden_all, down, preferred_element_type=jnp.float32)
        total = term if total is None else total + term
    if pairwise(ngx):
        result = fanout_reduce_scatter(total, "gx", ngx, gx_levels[::-1])
    else:
        result = lax.psum_scatter(total, "gx", scatter_dimension=0, tiled=True)
    return result.astype(jnp.bfloat16)


def solution(mesh):
    in_specs = (P(("groups", "gx"), "gy"), P("gy"), P("gy", "gx"), P("gy", "gx"), P("gx", "gy"))
    out_specs = P(("groups", "gx"), "gy")
    return jax.shard_map(local, mesh=mesh, in_specs=in_specs, out_specs=out_specs, check_vma=False)
```

```python
import jax
import jax.numpy as jnp
from jax import lax
from jax.experimental import pallas as pl
from jax.experimental.pallas import tpu as pltpu
from jax.sharding import PartitionSpec as P


epsilon = 1e-06

EXCHANGE_MAX = 8
CHUNKS = 2


def pairwise(n):
    return n <= EXCHANGE_MAX and n & (n - 1) == 0


def exchange(x, axis, n, s):
    return lax.ppermute(x, axis, [(a, a ^ (1 << s)) for a in range(n)])


def xor_reduce_scatter(parts, axis, n, dim, bits):
    me = lax.axis_index(axis)
    for s in bits:
        bit = (me >> s) & 1
        half = parts[0].shape[dim] // 2
        keep = [lax.dynamic_slice_in_dim(p, bit * half, half, axis=dim) for p in parts]
        send = [lax.dynamic_slice_in_dim(p, (1 - bit) * half, half, axis=dim) for p in parts]
        got = exchange(jnp.stack(send), axis, n, s)
        parts = [k + got[i] for i, k in enumerate(keep)]
    return parts


def xor_all_gather(x, axis, n, dim, bits):
    me = lax.axis_index(axis)
    for s in bits:
        other = exchange(x, axis, n, s)
        low = jnp.concatenate([x, other], axis=dim)
        high = jnp.concatenate([other, x], axis=dim)
        x = jnp.where(((me >> s) & 1) == 0, low, high)
    return x


def xor_all_reduce(x, axis, n):
    for s in range(n.bit_length() - 1):
        x = x + exchange(x, axis, n, s)
    return x


def gathered_position(d, bits):
    return sum(((d >> s) & 1) << t for t, s in enumerate(bits))


def fanout_reduce_scatter(x, axis, n, bits):
    me = lax.axis_index(axis)
    rows = x.shape[0] // n
    own = lax.dynamic_slice_in_dim(x, gathered_position(me, bits) * rows, rows, axis=0)
    for k in range(1, n):
        block = lax.dynamic_slice_in_dim(x, gathered_position(me ^ k, bits) * rows, rows, axis=0)
        own = own + lax.ppermute(block, axis, [(a, a ^ k) for a in range(n)])
    return own


def fanout_all_gather(x, axis, n, bits):
    me = lax.axis_index(axis)
    rows = x.shape[0]
    out = jnp.zeros((n * rows,) + x.shape[1:], x.dtype)
    for k in range(n):
        block = x if k == 0 else lax.ppermute(x, axis, [(a, a ^ k) for a in range(n)])
        out = lax.dynamic_update_slice_in_dim(out, block, gathered_position(me ^ k, bits) * rows, axis=0)
    return out


def fanout_all_reduce(x, axis, n):
    me = lax.axis_index(axis)
    got = jnp.stack([x] + [lax.ppermute(x, axis, [(a, a ^ k) for a in range(n)]) for k in range(1, n)])
    ordered = jnp.take(got, jnp.arange(n) ^ me, axis=0)
    return jnp.sum(ordered, axis=0)


def rows_to_vmem(w, start, count):
    size = count * w.shape[1] * w.dtype.itemsize

    def kernel(src, dst, sem):
        copy = pltpu.make_async_copy(src.at[pl.ds(start, count), :], dst, sem)
        copy.start()
        copy.wait()

    return pl.pallas_call(
        kernel,
        out_shape=jax.ShapeDtypeStruct((count, w.shape[1]), w.dtype),
        in_specs=[pl.BlockSpec(memory_space=pl.ANY)],
        out_specs=pl.BlockSpec(memory_space=pltpu.VMEM),
        scratch_shapes=[pltpu.SemaphoreType.DMA(())],
        cost_estimate=pl.CostEstimate(flops=0, transcendentals=0, bytes_accessed=2 * size),
        compiler_params=pltpu.CompilerParams(vmem_limit_bytes=size + (2 << 20)),
    )(pltpu.with_memory_space_constraint(w, pltpu.HBM))


def local(tokens, norm_gain, w_gate, w_up, w_down):
    ngx = lax.axis_size("gx")
    ngy = lax.axis_size("gy")
    features = tokens.shape[1] * ngy
    gx_levels = list(range(ngx.bit_length() - 1))
    if pairwise(ngx):
        raw = fanout_all_gather(tokens, "gx", ngx, gx_levels[::-1])
    else:
        raw = lax.all_gather(tokens, "gx", axis=0, tiled=True)
    values = raw.astype(jnp.float32)
    local_sq = jnp.sum(values * values, axis=1)
    if pairwise(ngy):
        total_sq = xor_all_reduce(local_sq, "gy", ngy)
    else:
        total_sq = lax.psum(local_sq, "gy")
    inverse = lax.rsqrt(total_sq / features + epsilon)
    piece = (values * inverse[:, None] * norm_gain[None, :]).astype(jnp.bfloat16)
    rows = piece.shape[0]

    width = w_gate.shape[1]
    chunks = CHUNKS if width % (CHUNKS * ngy * 128) == 0 else 1
    step = width // chunks
    gy_levels = list(range(ngy.bit_length() - 1))
    total = None
    for c in range(chunks):
        cols = slice(c * step, (c + 1) * step)
        gate_part = jnp.dot(piece, w_gate[:, cols], preferred_element_type=jnp.float32)
        up_part = jnp.dot(piece, w_up[:, cols], preferred_element_type=jnp.float32)
        if pairwise(ngy):
            first = xor_reduce_scatter([gate_part, up_part], "gy", ngy, 1, gy_levels[:1])
            if c == 0:
                source, _ = lax.optimization_barrier((w_down, first[0]))
                staged = [rows_to_vmem(source, 0, step)]
            gate, up = xor_reduce_scatter(first, "gy", ngy, 1, gy_levels[1:])
            if c == 0:
                for k in range(1, chunks):
                    source, _ = lax.optimization_barrier((w_down, gate))
                    staged.append(rows_to_vmem(source, k * step, step))
        else:
            gate = lax.psum_scatter(gate_part, "gy", scatter_dimension=1, tiled=True)
            up = lax.psum_scatter(up_part, "gy", scatter_dimension=1, tiled=True)
        hidden = (jax.nn.silu(gate) * up).astype(jnp.bfloat16)
        if pairwise(ngy):
            hidden_all = xor_all_gather(hidden, "gy", ngy, 1, gy_levels[::-1])
        else:
            hidden_all = lax.all_gather(hidden, "gy", axis=1, tiled=True)
        down = staged[c] if pairwise(ngy) else w_down[cols, :]
        term = jnp.dot(hidden_all, down, preferred_element_type=jnp.float32)
        total = term if total is None else total + term
    if pairwise(ngx):
        result = fanout_reduce_scatter(total, "gx", ngx, gx_levels[::-1])
    else:
        result = lax.psum_scatter(total, "gx", scatter_dimension=0, tiled=True)
    return result.astype(jnp.bfloat16)


def solution(mesh):
    in_specs = (P(("groups", "gx"), "gy"), P("gy"), P("gy", "gx"), P("gy", "gx"), P("gx", "gy"))
    out_specs = P(("groups", "gx"), "gy")
    return jax.shard_map(local, mesh=mesh, in_specs=in_specs, out_specs=out_specs, check_vma=False)
```

```python
import jax
import jax.numpy as jnp
from jax import lax
from jax.experimental import pallas as pl
from jax.experimental.pallas import tpu as pltpu
from jax.sharding import PartitionSpec as P


epsilon = 1e-06

EXCHANGE_MAX = 8
CHUNKS = 2


def pairwise(n):
    return n <= EXCHANGE_MAX and n & (n - 1) == 0


def exchange(x, axis, n, s):
    return lax.ppermute(x, axis, [(a, a ^ (1 << s)) for a in range(n)])


def xor_reduce_scatter(parts, axis, n, dim, bits):
    me = lax.axis_index(axis)
    for s in bits:
        bit = (me >> s) & 1
        half = parts[0].shape[dim] // 2
        keep = [lax.dynamic_slice_in_dim(p, bit * half, half, axis=dim) for p in parts]
        send = [lax.dynamic_slice_in_dim(p, (1 - bit) * half, half, axis=dim) for p in parts]
        got = exchange(jnp.stack(send), axis, n, s)
        parts = [k + got[i] for i, k in enumerate(keep)]
    return parts


def xor_all_gather(x, axis, n, dim, bits):
    me = lax.axis_index(axis)
    for s in bits:
        other = exchange(x, axis, n, s)
        low = jnp.concatenate([x, other], axis=dim)
        high = jnp.concatenate([other, x], axis=dim)
        x = jnp.where(((me >> s) & 1) == 0, low, high)
    return x


def xor_all_reduce(x, axis, n):
    for s in range(n.bit_length() - 1):
        x = x + exchange(x, axis, n, s)
    return x


def gathered_position(d, bits):
    return sum(((d >> s) & 1) << t for t, s in enumerate(bits))


def fanout_reduce_scatter(x, axis, n, bits):
    me = lax.axis_index(axis)
    rows = x.shape[0] // n
    own = lax.dynamic_slice_in_dim(x, gathered_position(me, bits) * rows, rows, axis=0)
    for k in range(1, n):
        block = lax.dynamic_slice_in_dim(x, gathered_position(me ^ k, bits) * rows, rows, axis=0)
        own = own + lax.ppermute(block, axis, [(a, a ^ k) for a in range(n)])
    return own


def fanout_all_gather(x, axis, n, bits):
    me = lax.axis_index(axis)
    rows = x.shape[0]
    out = jnp.zeros((n * rows,) + x.shape[1:], x.dtype)
    for k in range(n):
        block = x if k == 0 else lax.ppermute(x, axis, [(a, a ^ k) for a in range(n)])
        out = lax.dynamic_update_slice_in_dim(out, block, gathered_position(me ^ k, bits) * rows, axis=0)
    return out


def fanout_all_reduce(x, axis, n):
    total = x
    for k in range(1, n):
        total = total + lax.ppermute(x, axis, [(a, a ^ k) for a in range(n)])
    return total


def rows_to_vmem(w, start, count):
    size = count * w.shape[1] * w.dtype.itemsize

    def kernel(src, dst, sem):
        copy = pltpu.make_async_copy(src.at[pl.ds(start, count), :], dst, sem)
        copy.start()
        copy.wait()

    return pl.pallas_call(
        kernel,
        out_shape=jax.ShapeDtypeStruct((count, w.shape[1]), w.dtype),
        in_specs=[pl.BlockSpec(memory_space=pl.ANY)],
        out_specs=pl.BlockSpec(memory_space=pltpu.VMEM),
        scratch_shapes=[pltpu.SemaphoreType.DMA(())],
        cost_estimate=pl.CostEstimate(flops=0, transcendentals=0, bytes_accessed=2 * size),
        compiler_params=pltpu.CompilerParams(vmem_limit_bytes=size + (2 << 20)),
    )(pltpu.with_memory_space_constraint(w, pltpu.HBM))


def local(tokens, norm_gain, w_gate, w_up, w_down):
    ngx = lax.axis_size("gx")
    ngy = lax.axis_size("gy")
    features = tokens.shape[1] * ngy
    gx_levels = list(range(ngx.bit_length() - 1))
    if pairwise(ngx):
        raw = fanout_all_gather(tokens, "gx", ngx, gx_levels[::-1])
    else:
        raw = lax.all_gather(tokens, "gx", axis=0, tiled=True)
    values = raw.astype(jnp.float32)
    local_sq = jnp.sum(values * values, axis=1)
    if pairwise(ngy):
        total_sq = fanout_all_reduce(local_sq, "gy", ngy)
    else:
        total_sq = lax.psum(local_sq, "gy")
    inverse = lax.rsqrt(total_sq / features + epsilon)
    piece = (values * inverse[:, None] * norm_gain[None, :]).astype(jnp.bfloat16)
    rows = piece.shape[0]

    width = w_gate.shape[1]
    chunks = CHUNKS if width % (CHUNKS * ngy * 128) == 0 else 1
    step = width // chunks
    gy_levels = list(range(ngy.bit_length() - 1))
    total = None
    for c in range(chunks):
        cols = slice(c * step, (c + 1) * step)
        gate_part = jnp.dot(piece, w_gate[:, cols], preferred_element_type=jnp.float32)
        up_part = jnp.dot(piece, w_up[:, cols], preferred_element_type=jnp.float32)
        if pairwise(ngy):
            first = xor_reduce_scatter([gate_part, up_part], "gy", ngy, 1, gy_levels[:1])
            if c == 0:
                source, _ = lax.optimization_barrier((w_down, first[0]))
                staged = [rows_to_vmem(source, 0, step)]
            gate, up = xor_reduce_scatter(first, "gy", ngy, 1, gy_levels[1:])
            if c == 0:
                for k in range(1, chunks):
                    source, _ = lax.optimization_barrier((w_down, gate))
                    staged.append(rows_to_vmem(source, k * step, step))
        else:
            gate = lax.psum_scatter(gate_part, "gy", scatter_dimension=1, tiled=True)
            up = lax.psum_scatter(up_part, "gy", scatter_dimension=1, tiled=True)
        hidden = (jax.nn.silu(gate) * up).astype(jnp.bfloat16)
        if pairwise(ngy):
            hidden_all = xor_all_gather(hidden, "gy", ngy, 1, gy_levels[::-1])
        else:
            hidden_all = lax.all_gather(hidden, "gy", axis=1, tiled=True)
        down = staged[c] if pairwise(ngy) else w_down[cols, :]
        term = jnp.dot(hidden_all, down, preferred_element_type=jnp.float32)
        total = term if total is None else total + term
    if pairwise(ngx):
        result = fanout_reduce_scatter(total, "gx", ngx, gx_levels[::-1])
    else:
        result = lax.psum_scatter(total, "gx", scatter_dimension=0, tiled=True)
    return result.astype(jnp.bfloat16)


def solution(mesh):
    in_specs = (P(("groups", "gx"), "gy"), P("gy"), P("gy", "gx"), P("gy", "gx"), P("gx", "gy"))
    out_specs = P(("groups", "gx"), "gy")
    return jax.shard_map(local, mesh=mesh, in_specs=in_specs, out_specs=out_specs, check_vma=False)
```

```python
import jax
import jax.numpy as jnp
from jax import lax
from jax.experimental import pallas as pl
from jax.experimental.pallas import tpu as pltpu
from jax.sharding import PartitionSpec as P


epsilon = 1e-06

EXCHANGE_MAX = 8
CHUNKS = 2


def pairwise(n):
    return n <= EXCHANGE_MAX and n & (n - 1) == 0


def exchange(x, axis, n, s):
    return lax.ppermute(x, axis, [(a, a ^ (1 << s)) for a in range(n)])


def xor_reduce_scatter(parts, axis, n, dim, bits):
    me = lax.axis_index(axis)
    for s in bits:
        bit = (me >> s) & 1
        half = parts[0].shape[dim] // 2
        keep = [lax.dynamic_slice_in_dim(p, bit * half, half, axis=dim) for p in parts]
        send = [lax.dynamic_slice_in_dim(p, (1 - bit) * half, half, axis=dim) for p in parts]
        got = exchange(jnp.stack(send), axis, n, s)
        parts = [k + got[i] for i, k in enumerate(keep)]
    return parts


def xor_all_gather(x, axis, n, dim, bits):
    me = lax.axis_index(axis)
    for s in bits:
        other = exchange(x, axis, n, s)
        low = jnp.concatenate([x, other], axis=dim)
        high = jnp.concatenate([other, x], axis=dim)
        x = jnp.where(((me >> s) & 1) == 0, low, high)
    return x


def xor_all_reduce(x, axis, n):
    for s in range(n.bit_length() - 1):
        x = x + exchange(x, axis, n, s)
    return x


def gathered_position(d, bits):
    return sum(((d >> s) & 1) << t for t, s in enumerate(bits))


def fanout_reduce_scatter(x, axis, n, bits):
    me = lax.axis_index(axis)
    rows = x.shape[0] // n
    own = lax.dynamic_slice_in_dim(x, gathered_position(me, bits) * rows, rows, axis=0)
    for k in range(n - 1, 0, -1):
        block = lax.dynamic_slice_in_dim(x, gathered_position(me ^ k, bits) * rows, rows, axis=0)
        own = own + lax.ppermute(block, axis, [(a, a ^ k) for a in range(n)])
    return own


def fanout_all_gather(x, axis, n, bits):
    me = lax.axis_index(axis)
    rows = x.shape[0]
    out = jnp.zeros((n * rows,) + x.shape[1:], x.dtype)
    for k in [0] + list(range(n - 1, 0, -1)):
        block = x if k == 0 else lax.ppermute(x, axis, [(a, a ^ k) for a in range(n)])
        out = lax.dynamic_update_slice_in_dim(out, block, gathered_position(me ^ k, bits) * rows, axis=0)
    return out


def fanout_all_reduce(x, axis, n):
    me = lax.axis_index(axis)
    got = jnp.stack([x] + [lax.ppermute(x, axis, [(a, a ^ k) for a in range(n)]) for k in range(1, n)])
    ordered = jnp.take(got, jnp.arange(n) ^ me, axis=0)
    return jnp.sum(ordered, axis=0)


def rows_to_vmem(w, start, count):
    size = count * w.shape[1] * w.dtype.itemsize

    def kernel(src, dst, sem):
        copy = pltpu.make_async_copy(src.at[pl.ds(start, count), :], dst, sem)
        copy.start()
        copy.wait()

    return pl.pallas_call(
        kernel,
        out_shape=jax.ShapeDtypeStruct((count, w.shape[1]), w.dtype),
        in_specs=[pl.BlockSpec(memory_space=pl.ANY)],
        out_specs=pl.BlockSpec(memory_space=pltpu.VMEM),
        scratch_shapes=[pltpu.SemaphoreType.DMA(())],
        cost_estimate=pl.CostEstimate(flops=0, transcendentals=0, bytes_accessed=2 * size),
        compiler_params=pltpu.CompilerParams(vmem_limit_bytes=size + (2 << 20)),
    )(pltpu.with_memory_space_constraint(w, pltpu.HBM))


def local(tokens, norm_gain, w_gate, w_up, w_down):
    ngx = lax.axis_size("gx")
    ngy = lax.axis_size("gy")
    features = tokens.shape[1] * ngy
    gx_levels = list(range(ngx.bit_length() - 1))
    if pairwise(ngx):
        raw = fanout_all_gather(tokens, "gx", ngx, gx_levels[::-1])
    else:
        raw = lax.all_gather(tokens, "gx", axis=0, tiled=True)
    values = raw.astype(jnp.float32)
    local_sq = jnp.sum(values * values, axis=1)
    if pairwise(ngy):
        total_sq = fanout_all_reduce(local_sq, "gy", ngy)
    else:
        total_sq = lax.psum(local_sq, "gy")
    inverse = lax.rsqrt(total_sq / features + epsilon)
    piece = (values * inverse[:, None] * norm_gain[None, :]).astype(jnp.bfloat16)
    rows = piece.shape[0]

    width = w_gate.shape[1]
    chunks = CHUNKS if width % (CHUNKS * ngy * 128) == 0 else 1
    step = width // chunks
    gy_levels = list(range(ngy.bit_length() - 1))
    total = None
    for c in range(chunks):
        cols = slice(c * step, (c + 1) * step)
        gate_part = jnp.dot(piece, w_gate[:, cols], preferred_element_type=jnp.float32)
        up_part = jnp.dot(piece, w_up[:, cols], preferred_element_type=jnp.float32)
        if pairwise(ngy):
            first = xor_reduce_scatter([gate_part, up_part], "gy", ngy, 1, gy_levels[:1])
            if c == 0:
                source, _ = lax.optimization_barrier((w_down, first[0]))
                staged = [rows_to_vmem(source, 0, step)]
            gate, up = xor_reduce_scatter(first, "gy", ngy, 1, gy_levels[1:])
            if c == 0:
                for k in range(1, chunks):
                    source, _ = lax.optimization_barrier((w_down, gate))
                    staged.append(rows_to_vmem(source, k * step, step))
        else:
            gate = lax.psum_scatter(gate_part, "gy", scatter_dimension=1, tiled=True)
            up = lax.psum_scatter(up_part, "gy", scatter_dimension=1, tiled=True)
        hidden = (jax.nn.silu(gate) * up).astype(jnp.bfloat16)
        if pairwise(ngy):
            hidden_all = xor_all_gather(hidden, "gy", ngy, 1, gy_levels[::-1])
        else:
            hidden_all = lax.all_gather(hidden, "gy", axis=1, tiled=True)
        down = staged[c] if pairwise(ngy) else w_down[cols, :]
        term = jnp.dot(hidden_all, down, preferred_element_type=jnp.float32)
        total = term if total is None else total + term
    if pairwise(ngx):
        result = fanout_reduce_scatter(total, "gx", ngx, gx_levels[::-1])
    else:
        result = lax.psum_scatter(total, "gx", scatter_dimension=0, tiled=True)
    return result.astype(jnp.bfloat16)


def solution(mesh):
    in_specs = (P(("groups", "gx"), "gy"), P("gy"), P("gy", "gx"), P("gy", "gx"), P("gx", "gy"))
    out_specs = P(("groups", "gx"), "gy")
    return jax.shard_map(local, mesh=mesh, in_specs=in_specs, out_specs=out_specs, check_vma=False)
```

```python
import jax
import jax.numpy as jnp
from jax import lax
from jax.experimental import pallas as pl
from jax.experimental.pallas import tpu as pltpu
from jax.sharding import PartitionSpec as P


epsilon = 1e-06

EXCHANGE_MAX = 8
CHUNKS = 2


def pairwise(n):
    return n <= EXCHANGE_MAX and n & (n - 1) == 0


def exchange(x, axis, n, s):
    return lax.ppermute(x, axis, [(a, a ^ (1 << s)) for a in range(n)])


def xor_reduce_scatter(parts, axis, n, dim, bits):
    me = lax.axis_index(axis)
    for s in bits:
        bit = (me >> s) & 1
        half = parts[0].shape[dim] // 2
        keep = [lax.dynamic_slice_in_dim(p, bit * half, half, axis=dim) for p in parts]
        send = [lax.dynamic_slice_in_dim(p, (1 - bit) * half, half, axis=dim) for p in parts]
        got = exchange(jnp.stack(send), axis, n, s)
        parts = [k + got[i] for i, k in enumerate(keep)]
    return parts


def xor_all_gather(x, axis, n, dim, bits):
    me = lax.axis_index(axis)
    for s in bits:
        other = exchange(x, axis, n, s)
        low = jnp.concatenate([x, other], axis=dim)
        high = jnp.concatenate([other, x], axis=dim)
        x = jnp.where(((me >> s) & 1) == 0, low, high)
    return x


def xor_all_reduce(x, axis, n):
    for s in range(n.bit_length() - 1):
        x = x + exchange(x, axis, n, s)
    return x


def gathered_position(d, bits):
    return sum(((d >> s) & 1) << t for t, s in enumerate(bits))


def fanout_reduce_scatter(x, axis, n, bits):
    me = lax.axis_index(axis)
    rows = x.shape[0] // n
    own = lax.dynamic_slice_in_dim(x, gathered_position(me, bits) * rows, rows, axis=0)
    for k in range(n - 1, 0, -1):
        block = lax.dynamic_slice_in_dim(x, gathered_position(me ^ k, bits) * rows, rows, axis=0)
        own = own + lax.ppermute(block, axis, [(a, a ^ k) for a in range(n)])
    return own


def fanout_all_gather(x, axis, n, bits):
    me = lax.axis_index(axis)
    rows = x.shape[0]
    out = jnp.zeros((n * rows,) + x.shape[1:], x.dtype)
    for k in [0] + list(range(n - 1, 0, -1)):
        block = x if k == 0 else lax.ppermute(x, axis, [(a, a ^ k) for a in range(n)])
        out = lax.dynamic_update_slice_in_dim(out, block, gathered_position(me ^ k, bits) * rows, axis=0)
    return out


def fanout_all_reduce(x, axis, n):
    me = lax.axis_index(axis)
    recv = {k: lax.ppermute(x, axis, [(a, a ^ k) for a in range(n)]) for k in range(n - 1, 0, -1)}
    got = jnp.stack([x] + [recv[k] for k in range(1, n)])
    ordered = jnp.take(got, jnp.arange(n) ^ me, axis=0)
    return jnp.sum(ordered, axis=0)


def rows_to_vmem(w, start, count):
    size = count * w.shape[1] * w.dtype.itemsize

    def kernel(src, dst, sem):
        copy = pltpu.make_async_copy(src.at[pl.ds(start, count), :], dst, sem)
        copy.start()
        copy.wait()

    return pl.pallas_call(
        kernel,
        out_shape=jax.ShapeDtypeStruct((count, w.shape[1]), w.dtype),
        in_specs=[pl.BlockSpec(memory_space=pl.ANY)],
        out_specs=pl.BlockSpec(memory_space=pltpu.VMEM),
        scratch_shapes=[pltpu.SemaphoreType.DMA(())],
        cost_estimate=pl.CostEstimate(flops=0, transcendentals=0, bytes_accessed=2 * size),
        compiler_params=pltpu.CompilerParams(vmem_limit_bytes=size + (2 << 20)),
    )(pltpu.with_memory_space_constraint(w, pltpu.HBM))


def local(tokens, norm_gain, w_gate, w_up, w_down):
    ngx = lax.axis_size("gx")
    ngy = lax.axis_size("gy")
    features = tokens.shape[1] * ngy
    gx_levels = list(range(ngx.bit_length() - 1))
    if pairwise(ngx):
        raw = fanout_all_gather(tokens, "gx", ngx, gx_levels[::-1])
    else:
        raw = lax.all_gather(tokens, "gx", axis=0, tiled=True)
    values = raw.astype(jnp.float32)
    local_sq = jnp.sum(values * values, axis=1)
    if pairwise(ngy):
        total_sq = fanout_all_reduce(local_sq, "gy", ngy)
    else:
        total_sq = lax.psum(local_sq, "gy")
    inverse = lax.rsqrt(total_sq / features + epsilon)
    piece = (values * inverse[:, None] * norm_gain[None, :]).astype(jnp.bfloat16)
    rows = piece.shape[0]

    width = w_gate.shape[1]
    chunks = CHUNKS if width % (CHUNKS * ngy * 128) == 0 else 1
    step = width // chunks
    gy_levels = list(range(ngy.bit_length() - 1))
    total = None
    for c in range(chunks):
        cols = slice(c * step, (c + 1) * step)
        gate_part = jnp.dot(piece, w_gate[:, cols], preferred_element_type=jnp.float32)
        up_part = jnp.dot(piece, w_up[:, cols], preferred_element_type=jnp.float32)
        if pairwise(ngy):
            first = xor_reduce_scatter([gate_part, up_part], "gy", ngy, 1, gy_levels[:1])
            if c == 0:
                source, _ = lax.optimization_barrier((w_down, first[0]))
                staged = [rows_to_vmem(source, 0, step)]
            gate, up = xor_reduce_scatter(first, "gy", ngy, 1, gy_levels[1:])
            if c == 0:
                for k in range(1, chunks):
                    source, _ = lax.optimization_barrier((w_down, gate))
                    staged.append(rows_to_vmem(source, k * step, step))
        else:
            gate = lax.psum_scatter(gate_part, "gy", scatter_dimension=1, tiled=True)
            up = lax.psum_scatter(up_part, "gy", scatter_dimension=1, tiled=True)
        hidden = (jax.nn.silu(gate) * up).astype(jnp.bfloat16)
        if pairwise(ngy):
            hidden_all = xor_all_gather(hidden, "gy", ngy, 1, gy_levels[::-1])
        else:
            hidden_all = lax.all_gather(hidden, "gy", axis=1, tiled=True)
        down = staged[c] if pairwise(ngy) else w_down[cols, :]
        term = jnp.dot(hidden_all, down, preferred_element_type=jnp.float32)
        total = term if total is None else total + term
    if pairwise(ngx):
        result = fanout_reduce_scatter(total, "gx", ngx, gx_levels[::-1])
    else:
        result = lax.psum_scatter(total, "gx", scatter_dimension=0, tiled=True)
    return result.astype(jnp.bfloat16)


def solution(mesh):
    in_specs = (P(("groups", "gx"), "gy"), P("gy"), P("gy", "gx"), P("gy", "gx"), P("gx", "gy"))
    out_specs = P(("groups", "gx"), "gy")
    return jax.shard_map(local, mesh=mesh, in_specs=in_specs, out_specs=out_specs, check_vma=False)
```
